256 devices in a mesh: owner: 64 (over z, y, core), neg: 4 (over x).
Axes of the slice: x: 4, y: 4, z: 8, core: 2. Of those that a mesh axis runs over, the one named last changes fastest.
Arguments:
- nbr_ids: int32 [2048, 50], P(('owner', 'neg')), may hold values from 0 to 262143, as said below
- visit_counts: int32 [2048, 50], P(('owner', 'neg')), may hold values from 1 to 32
- self_ids: int32 [2048], P(('owner', 'neg')), may hold values from 0 to 262143, as said below
- pos_ids: int32 [2048], P(('owner', 'neg')), may hold values from 0 to 262143, as said below
- neg_ids: int32 [2048, 128], P(('owner', 'neg')), may hold values from 0 to 262143, as said below
- table: bfloat16 [262144, 1024], P('owner'), may hold values from -6 to 6
- w_pool: bfloat16 [1024, 1024], replicated, may hold values from -0.1875 to 0.1875
- b_pool: float32 [1024], replicated, may hold values from -3 to 3
- w_conv: bfloat16 [2048, 1024], replicated, may hold values from -0.125 to 0.125
- b_conv: float32 [1024], replicated, may hold values from -3 to 3
Outputs:
- query_embed: float32 [2048, 1024], P(('owner', 'neg'))
- loss: float32 [], replicated
- grad_pool_w: float32 [1024, 1024], P('owner')
- grad_pool_b: float32 [1024], replicated
- grad_conv_w: float32 [2048, 1024], P('owner')
- grad_conv_b: float32 [1024], replicated
The draws below stay inside these ranges and needn't reach their ends.
Inputs may be any that keep to these rules, and one draw needn't show every extreme that they name: `nbr_ids`: page p belongs to owner p // 4096. Among the 400 entries of one device's rows, at most 16 belong to one owner. `neg_ids`: taken together, the self, positive and negative ids of one device's 8 queries name at most 36 pages of one owner. `self_ids`: counted with the negatives, see neg_ids. `pos_ids`: counted with the negatives, see neg_ids.
All inputs are finite; a program needn't handle non-finite values.
Results may differ from the reference program's by a relative error of at most 0.008.
Values may be sent and summed in bfloat16 or wider, within the bound.
No kernel may reach another device: no remote copies, remote signals or barrier semaphores. Data moves between devices by JAX's collectives and lax.ppermute only.
A program may use at most 128 MiB of HBM per device.

```python
import jax
import jax.numpy as jnp
from jax import lax

E = 1024
K = 50
NEGS = 128
Q_DEV = 8
CAP = 16
CAP2 = 36
PAGES_DEV = 4096
OWNERS = 64
PAGES = 262144
QUERIES = 2048


def owned_ids(key, tag_value, row_count, capacity):
    block_count = QUERIES // Q_DEV
    key_hot, key_order, key_row = jax.random.split(jax.random.fold_in(key, tag_value), 3)
    hot_owner = jax.random.randint(key_hot, (), 0, OWNERS)
    positions = jnp.arange(row_count, dtype=jnp.int32)
    owner_of = jnp.where(positions < capacity, hot_owner, (hot_owner + 1 + (positions - capacity) % (OWNERS - 1)) % OWNERS)
    order_keys = jax.random.randint(key_order, (block_count, row_count), 0, (2 ** 31 - 1) // row_count) * row_count + positions[None, :]
    shuffle = jnp.argsort(order_keys, axis=1)
    owners_shuffled = owner_of[shuffle]
    local_row = jax.random.randint(key_row, (block_count, row_count), 0, PAGES_DEV)
    return (owners_shuffled * PAGES_DEV + local_row).astype(jnp.int32)


def page_block(key):
    return owned_ids(key, 23, Q_DEV * (NEGS + 2), CAP2)


def draw_nbr_ids(key, part):
    return owned_ids(key, 11, Q_DEV * K, CAP).reshape(QUERIES, K)


def draw_self_ids(key, part):
    return page_block(key)[:, :Q_DEV].reshape(QUERIES)


def draw_pos_ids(key, part):
    return page_block(key)[:, Q_DEV:2 * Q_DEV].reshape(QUERIES)


def draw_neg_ids(key, part):
    return page_block(key)[:, 2 * Q_DEV:].reshape(QUERIES, NEGS)


def touch_ends(array, stream_key, least, largest):
    longest = array.shape.index(max(array.shape))
    spots = []
    for shift in (0, 1):
        where = [jax.random.randint(jax.random.fold_in(stream_key, axis), (), 0, length) for axis, length in enumerate(array.shape)]
        where[longest] = (where[longest] + shift) % array.shape[longest]
        spots.append(tuple(where))
    return array.at[spots[0]].set(least).at[spots[1]].set(largest)


def level_of(stream_key, dims, cuts, least, top_value):
    factor_of, own = 1.0, jax.random.fold_in(stream_key, 6)
    for axis_at, blocks in cuts:
        draws = jnp.exp(jax.random.uniform(jax.random.fold_in(own, axis_at), (blocks,), jnp.float32, least / len(cuts), top_value / len(cuts)))
        factor_of = factor_of * jnp.repeat(draws, dims[axis_at] // blocks).reshape([-1 if axis == axis_at else 1 for axis in range(len(dims))])
    return factor_of


def noise(own_key, extent, scale, most, shards=(), kind=jnp.bfloat16):
    loudness = level_of(own_key, extent, shards, -0.22, 0.18) if shards else 1.0
    values = jax.random.normal(own_key, extent, jnp.float32) * scale * loudness
    return jnp.minimum(jnp.maximum(values, -most), most).astype(kind)


def setup_inputs(seed: int = 0) -> dict:
    key_list = jax.random.split(jax.random.key(seed), 11)
    nbr_ids = draw_nbr_ids(jax.random.fold_in(key_list[10], 71), 0)
    visit_counts = touch_ends(jax.random.randint(key_list[1], (QUERIES, K), 1, 33), jax.random.fold_in(key_list[1], 1), 1, 32).astype(jnp.int32)
    self_ids = draw_self_ids(jax.random.fold_in(key_list[10], 71), 0)
    pos_ids = draw_pos_ids(jax.random.fold_in(key_list[10], 71), 0)
    neg_ids = draw_neg_ids(jax.random.fold_in(key_list[10], 71), 0)
    table = noise(key_list[5], (PAGES, E), 1.0, 6.0, ((0, 64),))
    w_pool = noise(key_list[6], (E, E), E ** -0.5, 0.1875)
    b_pool = noise(key_list[7], (E,), 0.5, 3.0, (), jnp.float32)
    w_conv = noise(key_list[8], (2 * E, E), (2 * E) ** -0.5, 0.125)
    b_conv = noise(key_list[9], (E,), 0.5, 3.0, (), jnp.float32)
    return dict(nbr_ids=nbr_ids, visit_counts=visit_counts, self_ids=self_ids, pos_ids=pos_ids, neg_ids=neg_ids, table=table, w_pool=w_pool, b_pool=b_pool, w_conv=w_conv, b_conv=b_conv)


margin_value = 0.5

def silu_slope(values):
    sig = jax.nn.sigmoid(values)
    return sig * (1.0 + values * (1.0 - sig))

def forward_backward(pooled, self_rows, pos_rows, neg_rows, w_pool, b_pool, w_conv, b_conv, grad_scale, loss_scale):
    width = w_pool.shape[0]
    highest = lax.Precision.HIGHEST
    pooled_b = pooled.astype(jnp.bfloat16)
    pre_pool = jnp.dot(pooled_b, w_pool, preferred_element_type=jnp.float32) + b_pool
    neighbour = jax.nn.silu(pre_pool).astype(jnp.bfloat16)
    joined = jnp.concatenate([self_rows, neighbour], axis=1)
    pre_conv = jnp.dot(joined, w_conv, preferred_element_type=jnp.float32) + b_conv
    hidden = jax.nn.silu(pre_conv)
    inverse = lax.rsqrt(lax.optimization_barrier(jnp.sum(hidden * hidden, axis=1, keepdims=True)) + 1e-05)
    embedding = hidden * inverse
    embed_f = embedding.astype(jnp.bfloat16).astype(jnp.float32)
    neg_f = neg_rows.astype(jnp.float32)
    pos_f = pos_rows.astype(jnp.float32)
    neg_scores = jnp.einsum('qe,qne->qn', embed_f, neg_f, precision=highest)
    pos_scores = lax.optimization_barrier(jnp.sum(embed_f * pos_f, axis=1))
    margins = neg_scores - pos_scores[:, None] + margin_value
    loss_part = jnp.sum(jax.nn.softplus(margins)) * loss_scale
    slope_f = jax.nn.sigmoid(margins).astype(jnp.bfloat16).astype(jnp.float32)
    d_embed = jnp.einsum('qn,qne->qe', slope_f, neg_f, precision=highest) - lax.optimization_barrier(jnp.sum(slope_f, axis=1, keepdims=True)) * pos_f
    radial = lax.optimization_barrier(jnp.sum(d_embed * embedding, axis=1, keepdims=True))
    d_pre_conv = silu_slope(pre_conv) * inverse * (d_embed - embedding * radial) * grad_scale
    d_conv_b = d_pre_conv.astype(jnp.bfloat16)
    grad_conv_w = jnp.dot(joined.T, d_conv_b, preferred_element_type=jnp.float32)
    grad_conv_b = lax.optimization_barrier(jnp.sum(d_pre_conv, axis=0))
    d_joined = jnp.dot(d_conv_b, w_conv.T, preferred_element_type=jnp.float32)
    d_pre_pool = silu_slope(pre_pool) * d_joined[:, width:]
    d_pool_b = d_pre_pool.astype(jnp.bfloat16)
    grad_pool_w = jnp.dot(pooled_b.T, d_pool_b, preferred_element_type=jnp.float32)
    grad_pool_b = lax.optimization_barrier(jnp.sum(d_pre_pool, axis=0))
    return (embedding, loss_part, grad_pool_w, grad_pool_b, grad_conv_w, grad_conv_b)

def reference(nbr_ids, visit_counts, self_ids, pos_ids, neg_ids, table, w_pool, b_pool, w_conv, b_conv):
    block_count = QUERIES // Q_DEV
    counts_f = visit_counts.astype(jnp.float32)
    weights = counts_f / lax.optimization_barrier(jnp.sum(counts_f, axis=1, keepdims=True))
    grad_scale = 1.0 / NEGS
    loss_scale = 1.0 / (QUERIES * NEGS)

    def one_block(inputs):
        nbr_blk, weight_blk, self_blk, pos_blk, neg_blk = inputs
        nbr_rows = table[nbr_blk]
        pooled = lax.optimization_barrier(jnp.sum(weight_blk[:, :, None] * nbr_rows.astype(jnp.float32), axis=1))
        return forward_backward(pooled, table[self_blk], table[pos_blk], table[neg_blk], w_pool, b_pool, w_conv, b_conv, grad_scale, loss_scale)
    results = lax.map(one_block, (nbr_ids.reshape(block_count, Q_DEV, K), weights.reshape(block_count, Q_DEV, K), self_ids.reshape(block_count, Q_DEV), pos_ids.reshape(block_count, Q_DEV), neg_ids.reshape(block_count, Q_DEV, NEGS)))
    embeds, losses, pool_ws, pool_bs, conv_ws, conv_bs = results
    return (embeds.reshape(QUERIES, E), jnp.sum(losses), lax.optimization_barrier(jnp.sum(pool_ws, axis=0)), lax.optimization_barrier(jnp.sum(pool_bs, axis=0)), lax.optimization_barrier(jnp.sum(conv_ws, axis=0)), lax.optimization_barrier(jnp.sum(conv_bs, axis=0)))
```

```python
import jax
import jax.numpy as jnp
from jax import lax
from jax.sharding import PartitionSpec as P

margin_value = 0.5


def silu_slope(values):
    sig = jax.nn.sigmoid(values)
    return sig * (1.0 + values * (1.0 - sig))


def forward(pooled, self_rows, w_pool, b_pool, w_conv, b_conv):
    pooled_b = pooled.astype(jnp.bfloat16)
    pre_pool = jnp.dot(pooled_b, w_pool, preferred_element_type=jnp.float32) + b_pool
    neighbour = jax.nn.silu(pre_pool).astype(jnp.bfloat16)
    joined = jnp.concatenate([self_rows, neighbour], axis=1)
    pre_conv = jnp.dot(joined, w_conv, preferred_element_type=jnp.float32) + b_conv
    hidden = jax.nn.silu(pre_conv)
    inverse = lax.rsqrt(jnp.sum(hidden * hidden, axis=1, keepdims=True) + 1e-05)
    embedding = hidden * inverse
    return (pooled_b, pre_pool, joined, pre_conv, inverse, embedding)


def margin_terms(neg_scores, pos_scores, loss_scale):
    margins = neg_scores - pos_scores[:, None] + margin_value
    loss_part = jnp.sum(jax.nn.softplus(margins)) * loss_scale
    slope_b = jax.nn.sigmoid(margins).astype(jnp.bfloat16)
    slope_total = jnp.sum(slope_b.astype(jnp.float32), axis=1, keepdims=True)
    return (loss_part, slope_b, slope_total)


def backward_factors(d_embed, embedding, inverse, pre_conv, pre_pool, w_conv, grad_scale):
    width = embedding.shape[1]
    radial = jnp.sum(d_embed * embedding, axis=1, keepdims=True)
    d_pre_conv = silu_slope(pre_conv) * inverse * (d_embed - embedding * radial) * grad_scale
    d_conv_b = d_pre_conv.astype(jnp.bfloat16)
    grad_conv_b = jnp.sum(d_pre_conv, axis=0)
    d_neighbour = lax.dot_general(
        d_conv_b, w_conv[width:], (((1,), (1,)), ((), ())), preferred_element_type=jnp.float32
    )
    d_pre_pool = silu_slope(pre_pool) * d_neighbour
    d_pool_b = d_pre_pool.astype(jnp.bfloat16)
    grad_pool_b = jnp.sum(d_pre_pool, axis=0)
    return (d_conv_b, d_pool_b, grad_pool_b, grad_conv_b)


def weight_grads(joined, pooled_b, d_conv_b, d_pool_b):
    owners = lax.axis_size("owner")
    queries = joined.shape[0]
    conv_rows = joined.shape[1] // owners
    pool_rows = pooled_b.shape[1] // owners
    left = jnp.concatenate(
        [
            joined.reshape(queries, owners, conv_rows).transpose(1, 0, 2),
            pooled_b.reshape(queries, owners, pool_rows).transpose(1, 0, 2),
        ],
        axis=2,
    )
    left = lax.all_to_all(left, "owner", split_axis=0, concat_axis=0, tiled=True)
    left = left.reshape(owners * queries, conv_rows + pool_rows)
    right = lax.all_gather(
        jnp.concatenate([d_conv_b, d_pool_b], axis=1), "owner", axis=0, tiled=True
    )
    contract_rows = (((0,), (0,)), ((), ()))
    conv_width = d_conv_b.shape[1]
    conv_part = lax.dot_general(
        left[:, :conv_rows], right[:, :conv_width], contract_rows,
        preferred_element_type=jnp.float32,
    )
    pool_part = lax.dot_general(
        left[:, conv_rows:], right[:, conv_width:], contract_rows,
        preferred_element_type=jnp.float32,
    )
    return pool_part, conv_part


def bucket(page_list, owners, rows_per):
    owner_of = page_list // rows_per
    local_row = page_list - owner_of * rows_per
    one_hot = (owner_of[:, None] == jnp.arange(owners, dtype=jnp.int32)[None, :]).astype(jnp.int32)
    slot_of = jnp.sum((jnp.cumsum(one_hot, axis=0) - 1) * one_hot, axis=1)
    return (owner_of, slot_of, local_row)


def local(nbr_ids, visit_counts, self_ids, pos_ids, neg_ids, table, w_pool, b_pool, w_conv, b_conv):
    owners = lax.axis_size("owner")
    groups = lax.axis_size("neg")
    rows_per = table.shape[0]
    width = table.shape[1]
    queries, fan_count = nbr_ids.shape
    neg_count = neg_ids.shape[1]
    counts_f = visit_counts.astype(jnp.float32)
    weights = counts_f / jnp.sum(counts_f, axis=1, keepdims=True)
    flat_ids = nbr_ids.reshape(-1)
    capacity = 2 * (flat_ids.shape[0] // owners) + 4
    owner_of, slot_of, local_row = bucket(flat_ids, owners, rows_per)
    requests = jnp.zeros((owners, capacity), jnp.int32).at[owner_of, slot_of].set(local_row)
    returned = lax.all_to_all(
        table[lax.all_to_all(requests, "owner", split_axis=0, concat_axis=0, tiled=True)],
        "owner",
        split_axis=0,
        concat_axis=0,
        tiled=True,
    )
    nbr_rows = returned[owner_of, slot_of].reshape(queries, fan_count, width)
    pooled = jnp.sum(weights[:, :, None] * nbr_rows.astype(jnp.float32), axis=1)
    page_cap = 2 * (queries * (neg_count + 2) // owners) + 4
    total_queries = queries * owners * groups
    grad_scale = 1.0 / neg_count
    loss_scale = 1.0 / (total_queries * neg_count)
    page_list = jnp.concatenate([self_ids, pos_ids, neg_ids.reshape(-1)])
    page_owner, page_slot, page_row = bucket(page_list, owners, rows_per)
    page_requests = jnp.zeros((owners, page_cap), jnp.int32).at[page_owner, page_slot].set(page_row)
    page_back = lax.all_to_all(
        table[lax.all_to_all(page_requests, "owner", split_axis=0, concat_axis=0, tiled=True)],
        "owner",
        split_axis=0,
        concat_axis=0,
        tiled=True,
    )
    page_rows = page_back[page_owner, page_slot]
    self_rows = page_rows[:queries]
    pos_rows = page_rows[queries : 2 * queries]
    neg_rows = page_rows[2 * queries :].reshape(queries, neg_count, width)
    pooled_b, pre_pool, joined, pre_conv, inverse, embedding = forward(
        pooled, self_rows, w_pool, b_pool, w_conv, b_conv
    )
    embed_b = embedding.astype(jnp.bfloat16)
    neg_scores = jnp.einsum("qe,qne->qn", embed_b, neg_rows, preferred_element_type=jnp.float32)
    pos_scores = jnp.einsum("qe,qe->q", embed_b, pos_rows, preferred_element_type=jnp.float32)
    loss_part, slope_b, slope_total = margin_terms(neg_scores, pos_scores, loss_scale)
    d_embed = jnp.einsum(
        "qn,qne->qe", slope_b, neg_rows, preferred_element_type=jnp.float32
    ) - slope_total * pos_rows.astype(jnp.float32)
    d_conv_b, d_pool_b, pool_bgrad, conv_bgrad = backward_factors(
        d_embed, embedding, inverse, pre_conv, pre_pool, w_conv, grad_scale
    )
    pool_part, conv_part = weight_grads(joined, pooled_b, d_conv_b, d_pool_b)
    grad_pool_w, grad_conv_w = lax.psum((pool_part, conv_part), "neg")
    loss_sum, grad_pool_b, grad_conv_b = lax.psum(
        (loss_part, pool_bgrad, conv_bgrad), ("owner", "neg")
    )
    return (embedding, loss_sum, grad_pool_w, grad_pool_b, grad_conv_w, grad_conv_b)


def solution(mesh):
    return jax.shard_map(
        local,
        mesh=mesh,
        in_specs=(
            P(("owner", "neg"), None),
            P(("owner", "neg"), None),
            P(("owner", "neg")),
            P(("owner", "neg")),
            P(("owner", "neg"), None),
            P("owner", None),
            P(),
            P(),
            P(),
            P(),
        ),
        out_specs=(P(("owner", "neg"), None), P(), P("owner", None), P(), P("owner", None), P()),
        check_vma=False,
    )
```

```python
import jax
import jax.numpy as jnp
from jax import lax
from jax.sharding import PartitionSpec as P

margin_value = 0.5


def silu_slope(values):
    sig = jax.nn.sigmoid(values)
    return sig * (1.0 + values * (1.0 - sig))


def forward(pooled, self_rows, w_pool, b_pool, w_conv, b_conv):
    pooled_b = pooled.astype(jnp.bfloat16)
    pre_pool = jnp.dot(pooled_b, w_pool, preferred_element_type=jnp.float32) + b_pool
    neighbour = jax.nn.silu(pre_pool).astype(jnp.bfloat16)
    joined = jnp.concatenate([self_rows, neighbour], axis=1)
    pre_conv = jnp.dot(joined, w_conv, preferred_element_type=jnp.float32) + b_conv
    hidden = jax.nn.silu(pre_conv)
    inverse = lax.rsqrt(jnp.sum(hidden * hidden, axis=1, keepdims=True) + 1e-05)
    embedding = hidden * inverse
    return (pooled_b, pre_pool, joined, pre_conv, inverse, embedding)


def margin_terms(neg_scores, pos_scores, loss_scale):
    margins = neg_scores - pos_scores[:, None] + margin_value
    loss_part = jnp.sum(jax.nn.softplus(margins)) * loss_scale
    slope_b = jax.nn.sigmoid(margins).astype(jnp.bfloat16)
    slope_total = jnp.sum(slope_b.astype(jnp.float32), axis=1, keepdims=True)
    return (loss_part, slope_b, slope_total)


def backward_factors(d_embed, embedding, inverse, pre_conv, pre_pool, w_conv, grad_scale):
    width = embedding.shape[1]
    radial = jnp.sum(d_embed * embedding, axis=1, keepdims=True)
    d_pre_conv = silu_slope(pre_conv) * inverse * (d_embed - embedding * radial) * grad_scale
    d_conv_b = d_pre_conv.astype(jnp.bfloat16)
    grad_conv_b = jnp.sum(d_pre_conv, axis=0)
    d_neighbour = lax.dot_general(
        d_conv_b, w_conv[width:], (((1,), (1,)), ((), ())), preferred_element_type=jnp.float32
    )
    d_pre_pool = silu_slope(pre_pool) * d_neighbour
    d_pool_b = d_pre_pool.astype(jnp.bfloat16)
    grad_pool_b = jnp.sum(d_pre_pool, axis=0)
    return (d_conv_b, d_pool_b, grad_pool_b, grad_conv_b)


def weight_grads(joined, pooled_b, d_conv_b, d_pool_b, stats):
    owners = lax.axis_size("owner")
    queries = joined.shape[0]
    conv_rows = joined.shape[1] // owners
    pool_rows = pooled_b.shape[1] // owners
    left = jnp.concatenate(
        [
            joined.reshape(queries, owners, conv_rows).transpose(1, 0, 2),
            pooled_b.reshape(queries, owners, pool_rows).transpose(1, 0, 2),
        ],
        axis=2,
    )
    left = lax.all_to_all(left, "owner", split_axis=0, concat_axis=0, tiled=True)
    left = left.reshape(owners * queries, conv_rows + pool_rows)
    stats_hi = stats.astype(jnp.bfloat16)
    stats_lo = (stats - stats_hi.astype(jnp.float32)).astype(jnp.bfloat16)
    payload = jnp.concatenate([d_conv_b, d_pool_b], axis=1)
    payload = jnp.concatenate([payload, stats_hi, stats_lo], axis=0)
    gathered = lax.all_gather(payload, "owner", axis=0)
    right = gathered[:, :queries].reshape(owners * queries, payload.shape[1])
    stat_rows = stats.shape[0]
    stats_sum = jnp.sum(
        gathered[:, queries : queries + stat_rows].astype(jnp.float32)
        + gathered[:, queries + stat_rows :].astype(jnp.float32),
        axis=0,
    )
    contract_rows = (((0,), (0,)), ((), ()))
    conv_width = d_conv_b.shape[1]
    conv_part = lax.dot_general(
        left[:, :conv_rows], right[:, :conv_width], contract_rows,
        preferred_element_type=jnp.float32,
    )
    pool_part = lax.dot_general(
        left[:, conv_rows:], right[:, conv_width:], contract_rows,
        preferred_element_type=jnp.float32,
    )
    return pool_part, conv_part, stats_sum


def bucket(page_list, owners, rows_per, capacity):
    count = page_list.shape[0]
    owner_of = page_list // rows_per
    local_row = page_list - owner_of * rows_per
    one_hot = (owner_of[:, None] == jnp.arange(owners, dtype=jnp.int32)[None, :]).astype(jnp.bfloat16)
    positions = jnp.arange(count, dtype=jnp.int32)
    earlier = (positions[:, None] > positions[None, :]).astype(jnp.bfloat16)
    before = jnp.dot(earlier, one_hot, preferred_element_type=jnp.float32)
    slot_of = jnp.sum(before * one_hot.astype(jnp.float32), axis=1).astype(jnp.int32)
    flat = owner_of * capacity + slot_of
    select = (flat[:, None] == jnp.arange(owners * capacity, dtype=jnp.int32)[None, :]).astype(jnp.bfloat16)
    parts = jnp.stack([local_row // 64, local_row % 64]).astype(jnp.bfloat16)
    placed = jnp.dot(parts, select, preferred_element_type=jnp.float32).astype(jnp.int32)
    requests = (placed[0] * 64 + placed[1]).reshape(owners, capacity)
    return (owner_of, slot_of, requests)


def local(nbr_ids, visit_counts, self_ids, pos_ids, neg_ids, table, w_pool, b_pool, w_conv, b_conv):
    owners = lax.axis_size("owner")
    groups = lax.axis_size("neg")
    rows_per = table.shape[0]
    width = table.shape[1]
    queries, fan_count = nbr_ids.shape
    neg_count = neg_ids.shape[1]
    counts_f = visit_counts.astype(jnp.float32)
    weights = counts_f / jnp.sum(counts_f, axis=1, keepdims=True)
    flat_ids = nbr_ids.reshape(-1)
    capacity = 2 * (flat_ids.shape[0] // owners) + 4
    owner_of, slot_of, requests = bucket(flat_ids, owners, rows_per, capacity)
    page_cap = 2 * (queries * (neg_count + 2) // owners) + 4
    total_queries = queries * owners * groups
    grad_scale = 1.0 / neg_count
    loss_scale = 1.0 / (total_queries * neg_count)
    page_list = jnp.concatenate([self_ids, pos_ids, neg_ids.reshape(-1)])
    page_owner, page_slot, page_requests = bucket(page_list, owners, rows_per, page_cap)
    slots = capacity + page_cap
    all_requests = jnp.concatenate([requests, page_requests], axis=1)
    served = lax.all_to_all(all_requests, "owner", split_axis=0, concat_axis=0, tiled=True)
    returned = lax.all_to_all(table[served], "owner", split_axis=0, concat_axis=0, tiled=True)
    nbr_rows = returned[:, :capacity].reshape(owners * capacity, width)
    page_rows = returned[:, capacity:].reshape(owners * page_cap, width)
    nbr_flat = (owner_of * capacity + slot_of).reshape(queries, fan_count)
    nbr_slots = jnp.arange(owners * capacity, dtype=jnp.int32)
    pool_weights = jnp.sum(
        jnp.where(nbr_flat[:, :, None] == nbr_slots[None, None, :], weights[:, :, None], 0.0), axis=1
    )
    pooled = jnp.dot(
        pool_weights, nbr_rows.astype(jnp.float32), precision=lax.Precision.HIGHEST,
        preferred_element_type=jnp.float32,
    )
    page_flat = page_owner * page_cap + page_slot
    page_slots = jnp.arange(owners * page_cap, dtype=jnp.int32)
    self_flat = page_flat[:queries]
    pos_flat = page_flat[queries : 2 * queries]
    neg_flat = page_flat[2 * queries :].reshape(queries, neg_count)
    pick = (jnp.stack([self_flat, pos_flat])[:, :, None] == page_slots[None, None, :]).astype(jnp.bfloat16)
    picked = jnp.einsum("aqs,se->aqe", pick, page_rows, preferred_element_type=jnp.float32)
    self_rows = picked[0].astype(jnp.bfloat16)
    pos_rows = picked[1].astype(jnp.bfloat16)
    pooled_b, pre_pool, joined, pre_conv, inverse, embedding = forward(
        pooled, self_rows, w_pool, b_pool, w_conv, b_conv
    )
    embed_b = embedding.astype(jnp.bfloat16)
    slot_scores = lax.dot_general(
        embed_b, page_rows, (((1,), (1,)), ((), ())), preferred_element_type=jnp.float32
    )
    neg_scores = jnp.take_along_axis(slot_scores, neg_flat, axis=1)
    pos_scores = jnp.einsum("qe,qe->q", embed_b, pos_rows, preferred_element_type=jnp.float32)
    loss_part, slope_b, slope_total = margin_terms(neg_scores, pos_scores, loss_scale)
    slope_slots = jnp.sum(
        jnp.where(
            neg_flat[:, :, None] == page_slots[None, None, :],
            slope_b.astype(jnp.float32)[:, :, None],
            0.0,
        ),
        axis=1,
    ).astype(jnp.bfloat16)
    d_embed = jnp.dot(
        slope_slots, page_rows, preferred_element_type=jnp.float32
    ) - slope_total * pos_rows.astype(jnp.float32)
    d_conv_b, d_pool_b, pool_bgrad, conv_bgrad = backward_factors(
        d_embed, embedding, inverse, pre_conv, pre_pool, w_conv, grad_scale
    )
    loss_row = jnp.zeros((2 * width,), jnp.float32).at[0].set(loss_part)
    stats = jnp.stack([jnp.concatenate([conv_bgrad, pool_bgrad]), loss_row])
    pool_part, conv_part, stats_sum = weight_grads(joined, pooled_b, d_conv_b, d_pool_b, stats)
    grad_pool_w, grad_conv_w, stats_all = lax.psum((pool_part, conv_part, stats_sum), "neg")
    grad_conv_b = stats_all[0, :width]
    grad_pool_b = stats_all[0, width:]
    loss_sum = stats_all[1, 0]
    return (embedding, loss_sum, grad_pool_w, grad_pool_b, grad_conv_w, grad_conv_b)


def solution(mesh):
    return jax.shard_map(
        local,
        mesh=mesh,
        in_specs=(
            P(("owner", "neg"), None),
            P(("owner", "neg"), None),
            P(("owner", "neg")),
            P(("owner", "neg")),
            P(("owner", "neg"), None),
            P("owner", None),
            P(),
            P(),
            P(),
            P(),
        ),
        out_specs=(P(("owner", "neg"), None), P(), P("owner", None), P(), P("owner", None), P()),
        check_vma=False,
    )
```

```python
import jax
import jax.numpy as jnp
from jax import lax
from jax.sharding import PartitionSpec as P

margin_value = 0.5


def silu_slope(values):
    sig = jax.nn.sigmoid(values)
    return sig * (1.0 + values * (1.0 - sig))


def forward(pooled, self_rows, w_pool, b_pool, w_conv, b_conv):
    pooled_b = pooled.astype(jnp.bfloat16)
    pre_pool = jnp.dot(pooled_b, w_pool, preferred_element_type=jnp.float32) + b_pool
    neighbour = jax.nn.silu(pre_pool).astype(jnp.bfloat16)
    joined = jnp.concatenate([self_rows, neighbour], axis=1)
    pre_conv = jnp.dot(joined, w_conv, preferred_element_type=jnp.float32) + b_conv
    hidden = jax.nn.silu(pre_conv)
    inverse = lax.rsqrt(jnp.sum(hidden * hidden, axis=1, keepdims=True) + 1e-05)
    embedding = hidden * inverse
    return (pooled_b, pre_pool, joined, pre_conv, inverse, embedding)


def margin_terms(neg_scores, pos_scores, loss_scale):
    margins = neg_scores - pos_scores[:, None] + margin_value
    loss_part = jnp.sum(jax.nn.softplus(margins)) * loss_scale
    slope_b = jax.nn.sigmoid(margins).astype(jnp.bfloat16)
    slope_total = jnp.sum(slope_b.astype(jnp.float32), axis=1, keepdims=True)
    return (loss_part, slope_b, slope_total)


def backward_factors(d_embed, embedding, inverse, pre_conv, pre_pool, w_conv, grad_scale):
    width = embedding.shape[1]
    radial = jnp.sum(d_embed * embedding, axis=1, keepdims=True)
    d_pre_conv = silu_slope(pre_conv) * inverse * (d_embed - embedding * radial) * grad_scale
    d_conv_b = d_pre_conv.astype(jnp.bfloat16)
    grad_conv_b = jnp.sum(d_pre_conv, axis=0)
    d_neighbour = lax.dot_general(
        d_conv_b, w_conv[width:], (((1,), (1,)), ((), ())), preferred_element_type=jnp.float32
    )
    d_pre_pool = silu_slope(pre_pool) * d_neighbour
    d_pool_b = d_pre_pool.astype(jnp.bfloat16)
    grad_pool_b = jnp.sum(d_pre_pool, axis=0)
    return (d_conv_b, d_pool_b, grad_pool_b, grad_conv_b)


def weight_grads(joined, pooled_b, d_conv_b, d_pool_b, stats):
    owners = lax.axis_size("owner")
    queries = joined.shape[0]
    conv_rows = joined.shape[1] // owners
    pool_rows = pooled_b.shape[1] // owners
    left = jnp.concatenate(
        [
            joined.reshape(queries, owners, conv_rows).transpose(1, 0, 2),
            pooled_b.reshape(queries, owners, pool_rows).transpose(1, 0, 2),
        ],
        axis=2,
    )
    left = lax.all_to_all(left, "owner", split_axis=0, concat_axis=0, tiled=True)
    left = left.reshape(owners * queries, conv_rows + pool_rows)
    stats_hi = stats.astype(jnp.bfloat16)
    stats_lo = (stats - stats_hi.astype(jnp.float32)).astype(jnp.bfloat16)
    payload = jnp.concatenate([d_conv_b, d_pool_b], axis=1)
    payload = jnp.concatenate([payload, stats_hi, stats_lo], axis=0)
    gathered = lax.all_gather(payload, "owner", axis=0)
    right = gathered[:, :queries].reshape(owners * queries, payload.shape[1])
    stat_rows = stats.shape[0]
    stats_sum = jnp.sum(
        gathered[:, queries : queries + stat_rows].astype(jnp.float32)
        + gathered[:, queries + stat_rows :].astype(jnp.float32),
        axis=0,
    )
    contract_rows = (((0,), (0,)), ((), ()))
    conv_width = d_conv_b.shape[1]
    conv_part = lax.dot_general(
        left[:, :conv_rows], right[:, :conv_width], contract_rows,
        preferred_element_type=jnp.float32,
    )
    pool_part = lax.dot_general(
        left[:, conv_rows:], right[:, conv_width:], contract_rows,
        preferred_element_type=jnp.float32,
    )
    return pool_part, conv_part, stats_sum


def bucket(page_list, owners, rows_per, capacity):
    count = page_list.shape[0]
    owner_of = page_list // rows_per
    local_row = page_list - owner_of * rows_per
    one_hot = (owner_of[:, None] == jnp.arange(owners, dtype=jnp.int32)[None, :]).astype(jnp.bfloat16)
    positions = jnp.arange(count, dtype=jnp.int32)
    earlier = (positions[:, None] > positions[None, :]).astype(jnp.bfloat16)
    before = jnp.dot(earlier, one_hot, preferred_element_type=jnp.float32)
    slot_of = jnp.sum(before * one_hot.astype(jnp.float32), axis=1).astype(jnp.int32)
    flat = owner_of * capacity + slot_of
    select = (flat[:, None] == jnp.arange(owners * capacity, dtype=jnp.int32)[None, :]).astype(jnp.bfloat16)
    parts = jnp.stack([local_row // 64, local_row % 64]).astype(jnp.bfloat16)
    placed = jnp.dot(parts, select, preferred_element_type=jnp.float32).astype(jnp.int32)
    requests = (placed[0] * 64 + placed[1]).reshape(owners, capacity)
    return (owner_of, slot_of, requests)


def local(nbr_ids, visit_counts, self_ids, pos_ids, neg_ids, table, w_pool, b_pool, w_conv, b_conv):
    owners = lax.axis_size("owner")
    groups = lax.axis_size("neg")
    rows_per = table.shape[0]
    width = table.shape[1]
    queries, fan_count = nbr_ids.shape
    neg_count = neg_ids.shape[1]
    counts_f = visit_counts.astype(jnp.float32)
    weights = counts_f / jnp.sum(counts_f, axis=1, keepdims=True)
    flat_ids = nbr_ids.reshape(-1)
    capacity = 2 * (flat_ids.shape[0] // owners) + 4
    page_cap = 2 * (queries * (neg_count + 2) // owners) + 4
    capacity = -(-capacity // 8) * 8
    page_cap = -(-page_cap // 8) * 8
    total_queries = queries * owners * groups
    grad_scale = 1.0 / neg_count
    loss_scale = 1.0 / (total_queries * neg_count)
    owner_of, slot_of, requests = bucket(flat_ids, owners, rows_per, capacity)
    page_list = jnp.concatenate([self_ids, pos_ids, neg_ids.reshape(-1)])
    page_owner, page_slot, page_requests = bucket(page_list, owners, rows_per, page_cap)
    slots = capacity + page_cap
    all_requests = jnp.concatenate([requests, page_requests], axis=1)
    served = lax.all_to_all(all_requests, "owner", split_axis=0, concat_axis=0, tiled=True)
    returned = lax.all_to_all(
        table[served.reshape(-1)].reshape(owners, slots, width),
        "owner", split_axis=0, concat_axis=0, tiled=True,
    )
    nbr_rows = returned[:, :capacity].reshape(owners * capacity, width)
    page_rows = returned[:, capacity:].reshape(owners * page_cap, width)
    nbr_flat = (owner_of * capacity + slot_of).reshape(queries, fan_count)
    nbr_slots = jnp.arange(owners * capacity, dtype=jnp.int32)
    pool_weights = jnp.sum(
        jnp.where(nbr_flat[:, :, None] == nbr_slots[None, None, :], weights[:, :, None], 0.0), axis=1
    )
    pooled = jnp.dot(
        pool_weights, nbr_rows.astype(jnp.float32), precision=lax.Precision.HIGHEST,
        preferred_element_type=jnp.float32,
    )
    page_flat = page_owner * page_cap + page_slot
    page_slots = jnp.arange(owners * page_cap, dtype=jnp.int32)
    self_flat = page_flat[:queries]
    pos_flat = page_flat[queries : 2 * queries]
    neg_flat = page_flat[2 * queries :].reshape(queries, neg_count)
    pick = (jnp.stack([self_flat, pos_flat])[:, :, None] == page_slots[None, None, :]).astype(jnp.bfloat16)
    picked = jnp.einsum("aqs,se->aqe", pick, page_rows, preferred_element_type=jnp.float32)
    self_rows = picked[0].astype(jnp.bfloat16)
    pos_rows = picked[1].astype(jnp.bfloat16)
    pooled_b, pre_pool, joined, pre_conv, inverse, embedding = forward(
        pooled, self_rows, w_pool, b_pool, w_conv, b_conv
    )
    embed_b = embedding.astype(jnp.bfloat16)
    slot_scores = lax.dot_general(
        embed_b, page_rows, (((1,), (1,)), ((), ())), preferred_element_type=jnp.float32
    )
    neg_scores = jnp.take_along_axis(slot_scores, neg_flat, axis=1)
    pos_scores = jnp.einsum("qe,qe->q", embed_b, pos_rows, preferred_element_type=jnp.float32)
    loss_part, slope_b, slope_total = margin_terms(neg_scores, pos_scores, loss_scale)
    slope_slots = jnp.sum(
        jnp.where(
            neg_flat[:, :, None] == page_slots[None, None, :],
            slope_b.astype(jnp.float32)[:, :, None],
            0.0,
        ),
        axis=1,
    ).astype(jnp.bfloat16)
    d_embed = jnp.dot(
        slope_slots, page_rows, preferred_element_type=jnp.float32
    ) - slope_total * pos_rows.astype(jnp.float32)
    d_conv_b, d_pool_b, pool_bgrad, conv_bgrad = backward_factors(
        d_embed, embedding, inverse, pre_conv, pre_pool, w_conv, grad_scale
    )
    loss_row = jnp.zeros((2 * width,), jnp.float32).at[0].set(loss_part)
    stats = jnp.stack([jnp.concatenate([conv_bgrad, pool_bgrad]), loss_row])
    pool_part, conv_part, stats_sum = weight_grads(joined, pooled_b, d_conv_b, d_pool_b, stats)
    pool_rows = pool_part.shape[0]
    conv_rows = conv_part.shape[0]
    summed = lax.psum(
        jnp.concatenate([pool_part, conv_part, stats_sum.reshape(-1, width)], axis=0), "neg"
    )
    grad_pool_w = summed[:pool_rows]
    grad_conv_w = summed[pool_rows : pool_rows + conv_rows]
    stats_all = summed[pool_rows + conv_rows :].reshape(stats_sum.shape)
    grad_conv_b = stats_all[0, :width]
    grad_pool_b = stats_all[0, width:]
    loss_sum = stats_all[1, 0]
    return (embedding, loss_sum, grad_pool_w, grad_pool_b, grad_conv_w, grad_conv_b)


def solution(mesh):
    return jax.shard_map(
        local,
        mesh=mesh,
        in_specs=(
            P(("owner", "neg"), None),
            P(("owner", "neg"), None),
            P(("owner", "neg")),
            P(("owner", "neg")),
            P(("owner", "neg"), None),
            P("owner", None),
            P(),
            P(),
            P(),
            P(),
        ),
        out_specs=(P(("owner", "neg"), None), P(), P("owner", None), P(), P("owner", None), P()),
        check_vma=False,
    )
```

```python
import jax
import jax.numpy as jnp
from jax import lax
from jax.sharding import Mesh, PartitionSpec as P

margin_value = 0.5
OWNER = ("oz", "oy", "oc")


def silu_slope(values):
    sig = jax.nn.sigmoid(values)
    return sig * (1.0 + values * (1.0 - sig))


def forward(pooled, self_rows, w_pool, b_pool, w_conv, b_conv):
    pooled_b = pooled.astype(jnp.bfloat16)
    pre_pool = jnp.dot(pooled_b, w_pool, preferred_element_type=jnp.float32) + b_pool
    neighbour = jax.nn.silu(pre_pool).astype(jnp.bfloat16)
    joined = jnp.concatenate([self_rows, neighbour], axis=1)
    pre_conv = jnp.dot(joined, w_conv, preferred_element_type=jnp.float32) + b_conv
    hidden = jax.nn.silu(pre_conv)
    inverse = lax.rsqrt(jnp.sum(hidden * hidden, axis=1, keepdims=True) + 1e-05)
    embedding = hidden * inverse
    return (pooled_b, pre_pool, joined, pre_conv, inverse, embedding)


def margin_terms(neg_scores, pos_scores, loss_scale):
    margins = neg_scores - pos_scores[:, None] + margin_value
    loss_part = jnp.sum(jax.nn.softplus(margins)) * loss_scale
    slope_b = jax.nn.sigmoid(margins).astype(jnp.bfloat16)
    slope_total = jnp.sum(slope_b.astype(jnp.float32), axis=1, keepdims=True)
    return (loss_part, slope_b, slope_total)


def backward_factors(d_embed, embedding, inverse, pre_conv, pre_pool, w_conv, grad_scale):
    width = embedding.shape[1]
    radial = jnp.sum(d_embed * embedding, axis=1, keepdims=True)
    d_pre_conv = silu_slope(pre_conv) * inverse * (d_embed - embedding * radial) * grad_scale
    d_conv_b = d_pre_conv.astype(jnp.bfloat16)
    grad_conv_b = jnp.sum(d_pre_conv, axis=0)
    d_neighbour = lax.dot_general(
        d_conv_b, w_conv[width:], (((1,), (1,)), ((), ())), preferred_element_type=jnp.float32
    )
    d_pre_pool = silu_slope(pre_pool) * d_neighbour
    d_pool_b = d_pre_pool.astype(jnp.bfloat16)
    grad_pool_b = jnp.sum(d_pre_pool, axis=0)
    return (d_conv_b, d_pool_b, grad_pool_b, grad_conv_b)


def weight_grads(joined, pooled_b, d_conv_b, d_pool_b, stats):
    owners = lax.axis_size(OWNER)
    queries = joined.shape[0]
    conv_rows = joined.shape[1] // owners
    pool_rows = pooled_b.shape[1] // owners
    left = jnp.concatenate(
        [
            joined.reshape(queries, owners, conv_rows).transpose(1, 0, 2),
            pooled_b.reshape(queries, owners, pool_rows).transpose(1, 0, 2),
        ],
        axis=2,
    )
    left = lax.all_to_all(left, OWNER, split_axis=0, concat_axis=0, tiled=True)
    left = left.reshape(owners * queries, conv_rows + pool_rows)
    stats_hi = stats.astype(jnp.bfloat16)
    stats_lo = (stats - stats_hi.astype(jnp.float32)).astype(jnp.bfloat16)
    payload = jnp.concatenate([d_conv_b, d_pool_b], axis=1)
    payload = jnp.concatenate([payload, stats_hi, stats_lo], axis=0)
    gathered = payload
    for axis in OWNER[::-1]:
        gathered = lax.all_gather(gathered, axis, axis=0)
    gathered = gathered.reshape((owners,) + payload.shape)
    right = gathered[:, :queries].reshape(owners * queries, payload.shape[1])
    stat_rows = stats.shape[0]
    stats_sum = jnp.sum(
        gathered[:, queries : queries + stat_rows].astype(jnp.float32)
        + gathered[:, queries + stat_rows :].astype(jnp.float32),
        axis=0,
    )
    contract_rows = (((0,), (0,)), ((), ()))
    conv_width = d_conv_b.shape[1]
    conv_part = lax.dot_general(
        left[:, :conv_rows], right[:, :conv_width], contract_rows,
        preferred_element_type=jnp.float32,
    )
    pool_part = lax.dot_general(
        left[:, conv_rows:], right[:, conv_width:], contract_rows,
        preferred_element_type=jnp.float32,
    )
    return pool_part, conv_part, stats_sum


def bucket(page_list, owners, rows_per, capacity):
    count = page_list.shape[0]
    owner_of = page_list // rows_per
    local_row = page_list - owner_of * rows_per
    one_hot = (owner_of[:, None] == jnp.arange(owners, dtype=jnp.int32)[None, :]).astype(jnp.bfloat16)
    positions = jnp.arange(count, dtype=jnp.int32)
    earlier = (positions[:, None] > positions[None, :]).astype(jnp.bfloat16)
    before = jnp.dot(earlier, one_hot, preferred_element_type=jnp.float32)
    slot_of = jnp.sum(before * one_hot.astype(jnp.float32), axis=1).astype(jnp.int32)
    flat = owner_of * capacity + slot_of
    select = (flat[:, None] == jnp.arange(owners * capacity, dtype=jnp.int32)[None, :]).astype(jnp.bfloat16)
    parts = jnp.stack([local_row // 64, local_row % 64]).astype(jnp.bfloat16)
    placed = jnp.dot(parts, select, preferred_element_type=jnp.float32).astype(jnp.int32)
    requests = (placed[0] * 64 + placed[1]).reshape(owners, capacity)
    return (owner_of, slot_of, requests)


def local(nbr_ids, visit_counts, self_ids, pos_ids, neg_ids, table, w_pool, b_pool, w_conv, b_conv):
    owners = lax.axis_size(OWNER)
    groups = lax.axis_size("neg")
    rows_per = table.shape[0]
    width = table.shape[1]
    queries, fan_count = nbr_ids.shape
    neg_count = neg_ids.shape[1]
    counts_f = visit_counts.astype(jnp.float32)
    weights = counts_f / jnp.sum(counts_f, axis=1, keepdims=True)
    flat_ids = nbr_ids.reshape(-1)
    capacity = 2 * (flat_ids.shape[0] // owners) + 4
    page_cap = 2 * (queries * (neg_count + 2) // owners) + 4
    capacity = -(-capacity // 8) * 8
    page_cap = -(-page_cap // 8) * 8
    total_queries = queries * owners * groups
    grad_scale = 1.0 / neg_count
    loss_scale = 1.0 / (total_queries * neg_count)
    owner_of, slot_of, requests = bucket(flat_ids, owners, rows_per, capacity)
    page_list = jnp.concatenate([self_ids, pos_ids, neg_ids.reshape(-1)])
    page_owner, page_slot, page_requests = bucket(page_list, owners, rows_per, page_cap)
    slots = capacity + page_cap
    all_requests = jnp.concatenate([requests, page_requests], axis=1)
    served = lax.all_to_all(all_requests, OWNER, split_axis=0, concat_axis=0, tiled=True)
    returned = lax.all_to_all(
        table[served.reshape(-1)].reshape(owners, slots, width),
        OWNER, split_axis=0, concat_axis=0, tiled=True,
    )
    nbr_rows = returned[:, :capacity].reshape(owners * capacity, width)
    page_rows = returned[:, capacity:].reshape(owners * page_cap, width)
    nbr_flat = (owner_of * capacity + slot_of).reshape(queries, fan_count)
    nbr_slots = jnp.arange(owners * capacity, dtype=jnp.int32)
    pool_weights = jnp.sum(
        jnp.where(nbr_flat[:, :, None] == nbr_slots[None, None, :], weights[:, :, None], 0.0), axis=1
    )
    pooled = jnp.dot(
        pool_weights, nbr_rows.astype(jnp.float32), precision=lax.Precision.HIGHEST,
        preferred_element_type=jnp.float32,
    )
    page_flat = page_owner * page_cap + page_slot
    page_slots = jnp.arange(owners * page_cap, dtype=jnp.int32)
    self_flat = page_flat[:queries]
    pos_flat = page_flat[queries : 2 * queries]
    neg_flat = page_flat[2 * queries :].reshape(queries, neg_count)
    pick = (jnp.stack([self_flat, pos_flat])[:, :, None] == page_slots[None, None, :]).astype(jnp.bfloat16)
    picked = jnp.einsum("aqs,se->aqe", pick, page_rows, preferred_element_type=jnp.float32)
    self_rows = picked[0].astype(jnp.bfloat16)
    pos_rows = picked[1].astype(jnp.bfloat16)
    pooled_b, pre_pool, joined, pre_conv, inverse, embedding = forward(
        pooled, self_rows, w_pool, b_pool, w_conv, b_conv
    )
    embed_b = embedding.astype(jnp.bfloat16)
    slot_scores = lax.dot_general(
        embed_b, page_rows, (((1,), (1,)), ((), ())), preferred_element_type=jnp.float32
    )
    neg_scores = jnp.take_along_axis(slot_scores, neg_flat, axis=1)
    pos_scores = jnp.einsum("qe,qe->q", embed_b, pos_rows, preferred_element_type=jnp.float32)
    loss_part, slope_b, slope_total = margin_terms(neg_scores, pos_scores, loss_scale)
    slope_slots = jnp.sum(
        jnp.where(
            neg_flat[:, :, None] == page_slots[None, None, :],
            slope_b.astype(jnp.float32)[:, :, None],
            0.0,
        ),
        axis=1,
    ).astype(jnp.bfloat16)
    d_embed = jnp.dot(
        slope_slots, page_rows, preferred_element_type=jnp.float32
    ) - slope_total * pos_rows.astype(jnp.float32)
    d_conv_b, d_pool_b, pool_bgrad, conv_bgrad = backward_factors(
        d_embed, embedding, inverse, pre_conv, pre_pool, w_conv, grad_scale
    )
    loss_row = jnp.zeros((2 * width,), jnp.float32).at[0].set(loss_part)
    stats = jnp.stack([jnp.concatenate([conv_bgrad, pool_bgrad]), loss_row])
    pool_part, conv_part, stats_sum = weight_grads(joined, pooled_b, d_conv_b, d_pool_b, stats)
    pool_rows = pool_part.shape[0]
    conv_rows = conv_part.shape[0]
    summed = lax.psum(
        jnp.concatenate([pool_part, conv_part, stats_sum.reshape(-1, width)], axis=0), "neg"
    )
    grad_pool_w = summed[:pool_rows]
    grad_conv_w = summed[pool_rows : pool_rows + conv_rows]
    stats_all = summed[pool_rows + conv_rows :].reshape(stats_sum.shape)
    grad_conv_b = stats_all[0, :width]
    grad_pool_b = stats_all[0, width:]
    loss_sum = stats_all[1, 0]
    return (embedding, loss_sum, grad_pool_w, grad_pool_b, grad_conv_w, grad_conv_b)


def solution(mesh):
    owners, groups = mesh.devices.shape
    cores = 2
    rows_y = 4 if owners % (cores * 4) == 0 else 1
    fine = Mesh(
        mesh.devices.reshape(owners // (cores * rows_y), rows_y, cores, groups),
        OWNER + ("neg",),
    )
    spread = OWNER + ("neg",)
    return jax.shard_map(
        local,
        mesh=fine,
        in_specs=(
            P(spread, None),
            P(spread, None),
            P(spread),
            P(spread),
            P(spread, None),
            P(OWNER, None),
            P(),
            P(),
            P(),
            P(),
        ),
        out_specs=(P(spread, None), P(), P(OWNER, None), P(), P(OWNER, None), P()),
        check_vma=False,
    )
```

```python
import jax
import jax.numpy as jnp
from jax import lax
from jax.sharding import Mesh, PartitionSpec as P

margin_value = 0.5
OWNER = ("oz", "oy", "oc")


def silu_slope(values):
    sig = jax.nn.sigmoid(values)
    return sig * (1.0 + values * (1.0 - sig))


def forward(pooled, self_rows, w_pool, b_pool, w_conv, b_conv):
    pooled_b = pooled.astype(jnp.bfloat16)
    pre_pool = jnp.dot(pooled_b, w_pool, preferred_element_type=jnp.float32) + b_pool
    neighbour = jax.nn.silu(pre_pool).astype(jnp.bfloat16)
    joined = jnp.concatenate([self_rows, neighbour], axis=1)
    pre_conv = jnp.dot(joined, w_conv, preferred_element_type=jnp.float32) + b_conv
    hidden = jax.nn.silu(pre_conv)
    inverse = lax.rsqrt(jnp.sum(hidden * hidden, axis=1, keepdims=True) + 1e-05)
    embedding = hidden * inverse
    return (pooled_b, pre_pool, joined, pre_conv, inverse, embedding)


def margin_terms(neg_scores, pos_scores, loss_scale):
    margins = neg_scores - pos_scores[:, None] + margin_value
    loss_part = jnp.sum(jax.nn.softplus(margins)) * loss_scale
    slope_b = jax.nn.sigmoid(margins).astype(jnp.bfloat16)
    slope_total = jnp.sum(slope_b.astype(jnp.float32), axis=1, keepdims=True)
    return (loss_part, slope_b, slope_total)


def backward_factors(d_embed, embedding, inverse, pre_conv, pre_pool, w_conv, grad_scale):
    width = embedding.shape[1]
    radial = jnp.sum(d_embed * embedding, axis=1, keepdims=True)
    d_pre_conv = silu_slope(pre_conv) * inverse * (d_embed - embedding * radial) * grad_scale
    d_conv_b = d_pre_conv.astype(jnp.bfloat16)
    grad_conv_b = jnp.sum(d_pre_conv, axis=0)
    d_neighbour = lax.dot_general(
        d_conv_b, w_conv[width:], (((1,), (1,)), ((), ())), preferred_element_type=jnp.float32
    )
    d_pre_pool = silu_slope(pre_pool) * d_neighbour
    d_pool_b = d_pre_pool.astype(jnp.bfloat16)
    grad_pool_b = jnp.sum(d_pre_pool, axis=0)
    return (d_conv_b, d_pool_b, grad_pool_b, grad_conv_b)


def weight_grads(joined, pooled_b, d_conv_b, d_pool_b, stats):
    owners = lax.axis_size(OWNER)
    queries = joined.shape[0]
    conv_rows = joined.shape[1] // owners
    pool_rows = pooled_b.shape[1] // owners
    left = jnp.concatenate(
        [
            joined.reshape(queries, owners, conv_rows).transpose(1, 0, 2),
            pooled_b.reshape(queries, owners, pool_rows).transpose(1, 0, 2),
        ],
        axis=2,
    )
    left = lax.all_to_all(left, OWNER, split_axis=0, concat_axis=0, tiled=True)
    left = left.reshape(owners * queries, conv_rows + pool_rows)
    stats_hi = stats.astype(jnp.bfloat16)
    stats_lo = (stats - stats_hi.astype(jnp.float32)).astype(jnp.bfloat16)
    payload = jnp.concatenate([d_conv_b, d_pool_b], axis=1)
    payload = jnp.concatenate([payload, stats_hi, stats_lo], axis=0)
    gathered = payload
    for axis in OWNER[::-1]:
        gathered = lax.all_gather(gathered, axis, axis=0)
    gathered = gathered.reshape((owners,) + payload.shape)
    right = gathered[:, :queries].reshape(owners * queries, payload.shape[1])
    stat_rows = stats.shape[0]
    stats_sum = jnp.sum(
        gathered[:, queries : queries + stat_rows].astype(jnp.float32)
        + gathered[:, queries + stat_rows :].astype(jnp.float32),
        axis=0,
    )
    contract_rows = (((0,), (0,)), ((), ()))
    conv_width = d_conv_b.shape[1]
    conv_part = lax.dot_general(
        left[:, :conv_rows], right[:, :conv_width], contract_rows,
        preferred_element_type=jnp.float32,
    )
    pool_part = lax.dot_general(
        left[:, conv_rows:], right[:, conv_width:], contract_rows,
        preferred_element_type=jnp.float32,
    )
    return pool_part, conv_part, stats_sum


def pair_sum(values, groups):
    step = 1
    while step < groups:
        partner = lax.ppermute(values, "neg", [(i, i ^ step) for i in range(groups)])
        values = values + partner
        step *= 2
    return values


def bucket(page_list, owners, rows_per, capacity):
    count = page_list.shape[0]
    owner_of = page_list // rows_per
    local_row = page_list - owner_of * rows_per
    one_hot = (owner_of[:, None] == jnp.arange(owners, dtype=jnp.int32)[None, :]).astype(jnp.bfloat16)
    positions = jnp.arange(count, dtype=jnp.int32)
    earlier = (positions[:, None] > positions[None, :]).astype(jnp.bfloat16)
    before = jnp.dot(earlier, one_hot, preferred_element_type=jnp.float32)
    slot_of = jnp.sum(before * one_hot.astype(jnp.float32), axis=1).astype(jnp.int32)
    flat = owner_of * capacity + slot_of
    select = (flat[:, None] == jnp.arange(owners * capacity, dtype=jnp.int32)[None, :]).astype(jnp.bfloat16)
    parts = jnp.stack([local_row // 64, local_row % 64]).astype(jnp.bfloat16)
    placed = jnp.dot(parts, select, preferred_element_type=jnp.float32).astype(jnp.int32)
    requests = (placed[0] * 64 + placed[1]).reshape(owners, capacity)
    return (owner_of, slot_of, requests)


def local(nbr_ids, visit_counts, self_ids, pos_ids, neg_ids, table, w_pool, b_pool, w_conv, b_conv):
    owners = lax.axis_size(OWNER)
    groups = lax.axis_size("neg")
    rows_per = table.shape[0]
    width = table.shape[1]
    queries, fan_count = nbr_ids.shape
    neg_count = neg_ids.shape[1]
    counts_f = visit_counts.astype(jnp.float32)
    weights = counts_f / jnp.sum(counts_f, axis=1, keepdims=True)
    flat_ids = nbr_ids.reshape(-1)
    capacity = 2 * (flat_ids.shape[0] // owners) + 4
    page_cap = 2 * (queries * (neg_count + 2) // owners) + 4
    capacity = -(-capacity // 8) * 8
    page_cap = -(-page_cap // 8) * 8
    total_queries = queries * owners * groups
    grad_scale = 1.0 / neg_count
    loss_scale = 1.0 / (total_queries * neg_count)
    owner_of, slot_of, requests = bucket(flat_ids, owners, rows_per, capacity)
    page_list = jnp.concatenate([self_ids, pos_ids, neg_ids.reshape(-1)])
    page_owner, page_slot, page_requests = bucket(page_list, owners, rows_per, page_cap)
    slots = capacity + page_cap
    all_requests = jnp.concatenate([requests, page_requests], axis=1)
    served = lax.all_to_all(all_requests, OWNER, split_axis=0, concat_axis=0, tiled=True)
    returned = lax.all_to_all(
        table[served.reshape(-1)].reshape(owners, slots, width),
        OWNER, split_axis=0, concat_axis=0, tiled=True,
    )
    nbr_rows = returned[:, :capacity].reshape(owners * capacity, width)
    page_rows = returned[:, capacity:].reshape(owners * page_cap, width)
    nbr_flat = (owner_of * capacity + slot_of).reshape(queries, fan_count)
    nbr_slots = jnp.arange(owners * capacity, dtype=jnp.int32)
    pool_weights = jnp.sum(
        jnp.where(nbr_flat[:, :, None] == nbr_slots[None, None, :], weights[:, :, None], 0.0), axis=1
    )
    pooled = jnp.dot(
        pool_weights, nbr_rows.astype(jnp.float32), precision=lax.Precision.HIGHEST,
        preferred_element_type=jnp.float32,
    )
    page_flat = page_owner * page_cap + page_slot
    page_slots = jnp.arange(owners * page_cap, dtype=jnp.int32)
    self_flat = page_flat[:queries]
    pos_flat = page_flat[queries : 2 * queries]
    neg_flat = page_flat[2 * queries :].reshape(queries, neg_count)
    pick = (jnp.stack([self_flat, pos_flat])[:, :, None] == page_slots[None, None, :]).astype(jnp.bfloat16)
    picked = jnp.einsum("aqs,se->aqe", pick, page_rows, preferred_element_type=jnp.float32)
    self_rows = picked[0].astype(jnp.bfloat16)
    pos_rows = picked[1].astype(jnp.bfloat16)
    pooled_b, pre_pool, joined, pre_conv, inverse, embedding = forward(
        pooled, self_rows, w_pool, b_pool, w_conv, b_conv
    )
    embed_b = embedding.astype(jnp.bfloat16)
    slot_scores = lax.dot_general(
        embed_b, page_rows, (((1,), (1,)), ((), ())), preferred_element_type=jnp.float32
    )
    neg_scores = jnp.take_along_axis(slot_scores, neg_flat, axis=1)
    pos_scores = jnp.einsum("qe,qe->q", embed_b, pos_rows, preferred_element_type=jnp.float32)
    loss_part, slope_b, slope_total = margin_terms(neg_scores, pos_scores, loss_scale)
    slope_slots = jnp.sum(
        jnp.where(
            neg_flat[:, :, None] == page_slots[None, None, :],
            slope_b.astype(jnp.float32)[:, :, None],
            0.0,
        ),
        axis=1,
    ).astype(jnp.bfloat16)
    d_embed = jnp.dot(
        slope_slots, page_rows, preferred_element_type=jnp.float32
    ) - slope_total * pos_rows.astype(jnp.float32)
    d_conv_b, d_pool_b, pool_bgrad, conv_bgrad = backward_factors(
        d_embed, embedding, inverse, pre_conv, pre_pool, w_conv, grad_scale
    )
    loss_row = jnp.zeros((2 * width,), jnp.float32).at[0].set(loss_part)
    stats = jnp.stack([jnp.concatenate([conv_bgrad, pool_bgrad]), loss_row])
    pool_part, conv_part, stats_sum = weight_grads(joined, pooled_b, d_conv_b, d_pool_b, stats)
    pool_rows = pool_part.shape[0]
    conv_rows = conv_part.shape[0]
    summed = pair_sum(
        jnp.concatenate([pool_part, conv_part, stats_sum.reshape(-1, width)], axis=0), groups
    )
    grad_pool_w = summed[:pool_rows]
    grad_conv_w = summed[pool_rows : pool_rows + conv_rows]
    stats_all = summed[pool_rows + conv_rows :].reshape(stats_sum.shape)
    grad_conv_b = stats_all[0, :width]
    grad_pool_b = stats_all[0, width:]
    loss_sum = stats_all[1, 0]
    return (embedding, loss_sum, grad_pool_w, grad_pool_b, grad_conv_w, grad_conv_b)


def solution(mesh):
    owners, groups = mesh.devices.shape
    cores = 2
    rows_y = 4 if owners % (cores * 4) == 0 else 1
    fine = Mesh(
        mesh.devices.reshape(owners // (cores * rows_y), rows_y, cores, groups),
        OWNER + ("neg",),
    )
    spread = OWNER + ("neg",)
    return jax.shard_map(
        local,
        mesh=fine,
        in_specs=(
            P(spread, None),
            P(spread, None),
            P(spread),
            P(spread),
            P(spread, None),
            P(OWNER, None),
            P(),
            P(),
            P(),
            P(),
        ),
        out_specs=(P(spread, None), P(), P(OWNER, None), P(), P(OWNER, None), P()),
        check_vma=False,
    )
```

```python
import jax
import jax.numpy as jnp
from jax import lax
from jax.sharding import Mesh, PartitionSpec as P

margin_value = 0.5
OWNER = ("oz", "oy", "oc")


def silu_slope(values):
    sig = jax.nn.sigmoid(values)
    return sig * (1.0 + values * (1.0 - sig))


def forward(pooled, self_rows, w_pool, b_pool, w_conv, b_conv):
    pooled_b = pooled.astype(jnp.bfloat16)
    pre_pool = jnp.dot(pooled_b, w_pool, preferred_element_type=jnp.float32) + b_pool
    neighbour = jax.nn.silu(pre_pool).astype(jnp.bfloat16)
    joined = jnp.concatenate([self_rows, neighbour], axis=1)
    pre_conv = jnp.dot(joined, w_conv, preferred_element_type=jnp.float32) + b_conv
    hidden = jax.nn.silu(pre_conv)
    inverse = lax.rsqrt(jnp.sum(hidden * hidden, axis=1, keepdims=True) + 1e-05)
    embedding = hidden * inverse
    return (pooled_b, pre_pool, joined, pre_conv, inverse, embedding)


def margin_terms(neg_scores, pos_scores, loss_scale):
    margins = neg_scores - pos_scores[:, None] + margin_value
    loss_part = jnp.sum(jax.nn.softplus(margins)) * loss_scale
    slope_b = jax.nn.sigmoid(margins).astype(jnp.bfloat16)
    slope_total = jnp.sum(slope_b.astype(jnp.float32), axis=1, keepdims=True)
    return (loss_part, slope_b, slope_total)


def backward_factors(d_embed, embedding, inverse, pre_conv, pre_pool, w_conv, grad_scale):
    width = embedding.shape[1]
    radial = jnp.sum(d_embed * embedding, axis=1, keepdims=True)
    d_pre_conv = silu_slope(pre_conv) * inverse * (d_embed - embedding * radial) * grad_scale
    d_conv_b = d_pre_conv.astype(jnp.bfloat16)
    grad_conv_b = jnp.sum(d_pre_conv, axis=0)
    d_neighbour = lax.dot_general(
        d_conv_b, w_conv[width:], (((1,), (1,)), ((), ())), preferred_element_type=jnp.float32
    )
    d_pre_pool = silu_slope(pre_pool) * d_neighbour
    d_pool_b = d_pre_pool.astype(jnp.bfloat16)
    grad_pool_b = jnp.sum(d_pre_pool, axis=0)
    return (d_conv_b, d_pool_b, grad_pool_b, grad_conv_b)


def weight_grads(joined, pooled_b, d_conv_b, d_pool_b, stats):
    owners = lax.axis_size(OWNER)
    queries = joined.shape[0]
    conv_rows = joined.shape[1] // owners
    pool_rows = pooled_b.shape[1] // owners
    left = jnp.concatenate(
        [
            joined.reshape(queries, owners, conv_rows).transpose(1, 0, 2),
            pooled_b.reshape(queries, owners, pool_rows).transpose(1, 0, 2),
        ],
        axis=2,
    )
    left = lax.all_to_all(left, OWNER, split_axis=0, concat_axis=0, tiled=True)
    left = left.reshape(owners * queries, conv_rows + pool_rows)
    stats_hi = stats.astype(jnp.bfloat16)
    stats_lo = (stats - stats_hi.astype(jnp.float32)).astype(jnp.bfloat16)
    payload = jnp.concatenate([d_conv_b, d_pool_b], axis=1)
    payload = jnp.concatenate([payload, stats_hi, stats_lo], axis=0)
    gathered = payload
    for axis in OWNER[::-1]:
        gathered = lax.all_gather(gathered, axis, axis=0)
    gathered = gathered.reshape((owners,) + payload.shape)
    right = gathered[:, :queries].reshape(owners * queries, payload.shape[1])
    stat_rows = stats.shape[0]
    stats_sum = jnp.sum(
        gathered[:, queries : queries + stat_rows].astype(jnp.float32)
        + gathered[:, queries + stat_rows :].astype(jnp.float32),
        axis=0,
    )
    contract_rows = (((0,), (0,)), ((), ()))
    conv_width = d_conv_b.shape[1]
    conv_part = lax.dot_general(
        left[:, :conv_rows], right[:, :conv_width], contract_rows,
        preferred_element_type=jnp.float32,
    )
    pool_part = lax.dot_general(
        left[:, conv_rows:], right[:, conv_width:], contract_rows,
        preferred_element_type=jnp.float32,
    )
    return pool_part, conv_part, stats_sum


def pair_sum(values, groups):
    step = 1
    while step < groups:
        partner = lax.ppermute(values, "neg", [(i, i ^ step) for i in range(groups)])
        values = values + partner
        step *= 2
    return values


def bucket(page_list, owners, rows_per, capacity):
    count = page_list.shape[0]
    owner_of = page_list // rows_per
    local_row = page_list - owner_of * rows_per
    one_hot = (owner_of[:, None] == jnp.arange(owners, dtype=jnp.int32)[None, :]).astype(jnp.bfloat16)
    positions = jnp.arange(count, dtype=jnp.int32)
    earlier = (positions[:, None] > positions[None, :]).astype(jnp.bfloat16)
    before = jnp.dot(earlier, one_hot, preferred_element_type=jnp.float32)
    slot_of = jnp.sum(before * one_hot.astype(jnp.float32), axis=1).astype(jnp.int32)
    flat = owner_of * capacity + slot_of
    select = (flat[:, None] == jnp.arange(owners * capacity, dtype=jnp.int32)[None, :]).astype(jnp.bfloat16)
    parts = jnp.stack([local_row // 64, local_row % 64]).astype(jnp.bfloat16)
    placed = jnp.dot(parts, select, preferred_element_type=jnp.float32).astype(jnp.int32)
    requests = (placed[0] * 64 + placed[1]).reshape(owners, capacity)
    return (owner_of, slot_of, requests)


def local(nbr_ids, visit_counts, self_ids, pos_ids, neg_ids, table, w_pool, b_pool, w_conv, b_conv):
    owners = lax.axis_size(OWNER)
    groups = lax.axis_size("neg")
    rows_per = table.shape[0]
    width = table.shape[1]
    queries, fan_count = nbr_ids.shape
    neg_count = neg_ids.shape[1]
    counts_f = visit_counts.astype(jnp.float32)
    weights = counts_f / jnp.sum(counts_f, axis=1, keepdims=True)
    flat_ids = nbr_ids.reshape(-1)
    capacity = 2 * (flat_ids.shape[0] // owners) + 4
    page_cap = 2 * (queries * (neg_count + 2) // owners) + 4
    capacity = -(-capacity // 8) * 8
    page_cap = -(-page_cap // 8) * 8
    total_queries = queries * owners * groups
    grad_scale = 1.0 / neg_count
    loss_scale = 1.0 / (total_queries * neg_count)
    owner_of, slot_of, requests = bucket(flat_ids, owners, rows_per, capacity)
    page_list = jnp.concatenate([self_ids, pos_ids, neg_ids.reshape(-1)])
    page_owner, page_slot, page_requests = bucket(page_list, owners, rows_per, page_cap)
    slots = capacity + page_cap
    all_requests = jnp.concatenate([requests, page_requests], axis=1)
    served = lax.all_to_all(all_requests, OWNER, split_axis=0, concat_axis=0, tiled=True)
    returned = lax.all_to_all(
        table[served.reshape(-1)].reshape(owners, slots, width),
        OWNER, split_axis=0, concat_axis=0, tiled=True,
    )
    rows = returned.reshape(owners * slots, width)
    slot_ids = jnp.arange(owners * slots, dtype=jnp.int32)
    nbr_flat = (owner_of * slots + slot_of).reshape(queries, fan_count)
    page_flat = page_owner * slots + capacity + page_slot
    self_flat = page_flat[:queries]
    pos_flat = page_flat[queries : 2 * queries]
    neg_flat = page_flat[2 * queries :].reshape(queries, neg_count)
    pool_weights = jnp.sum(
        jnp.where(nbr_flat[:, :, None] == slot_ids[None, None, :], weights[:, :, None], 0.0), axis=1
    )
    part_1 = pool_weights.astype(jnp.bfloat16)
    rest_1 = pool_weights - part_1.astype(jnp.float32)
    part_2 = rest_1.astype(jnp.bfloat16)
    part_3 = (rest_1 - part_2.astype(jnp.float32)).astype(jnp.bfloat16)
    pick = (jnp.concatenate([self_flat, pos_flat])[:, None] == slot_ids[None, :]).astype(jnp.bfloat16)
    picked = jnp.dot(
        jnp.concatenate([part_1, part_2, part_3, pick], axis=0), rows,
        preferred_element_type=jnp.float32,
    )
    pooled = (picked[:queries] + picked[queries : 2 * queries]) + picked[2 * queries : 3 * queries]
    self_rows = picked[3 * queries : 4 * queries].astype(jnp.bfloat16)
    pos_rows = picked[4 * queries :].astype(jnp.bfloat16)
    pooled_b, pre_pool, joined, pre_conv, inverse, embedding = forward(
        pooled, self_rows, w_pool, b_pool, w_conv, b_conv
    )
    embed_b = embedding.astype(jnp.bfloat16)
    slot_scores = lax.dot_general(
        embed_b, rows, (((1,), (1,)), ((), ())), preferred_element_type=jnp.float32
    )
    neg_match = neg_flat[:, :, None] == slot_ids[None, None, :]
    neg_scores = jnp.sum(jnp.where(neg_match, slot_scores[:, None, :], 0.0), axis=2)
    pos_scores = jnp.einsum("qe,qe->q", embed_b, pos_rows, preferred_element_type=jnp.float32)
    loss_part, slope_b, slope_total = margin_terms(neg_scores, pos_scores, loss_scale)
    slope_slots = jnp.sum(
        jnp.where(neg_match, slope_b.astype(jnp.float32)[:, :, None], 0.0), axis=1
    ).astype(jnp.bfloat16)
    d_embed = jnp.dot(
        slope_slots, rows, preferred_element_type=jnp.float32
    ) - slope_total * pos_rows.astype(jnp.float32)
    d_conv_b, d_pool_b, pool_bgrad, conv_bgrad = backward_factors(
        d_embed, embedding, inverse, pre_conv, pre_pool, w_conv, grad_scale
    )
    loss_row = jnp.zeros((2 * width,), jnp.float32).at[0].set(loss_part)
    stats = jnp.stack([jnp.concatenate([conv_bgrad, pool_bgrad]), loss_row])
    pool_part, conv_part, stats_sum = weight_grads(joined, pooled_b, d_conv_b, d_pool_b, stats)
    pool_rows = pool_part.shape[0]
    conv_rows = conv_part.shape[0]
    summed = pair_sum(
        jnp.concatenate([pool_part, conv_part, stats_sum.reshape(-1, width)], axis=0), groups
    )
    grad_pool_w = summed[:pool_rows]
    grad_conv_w = summed[pool_rows : pool_rows + conv_rows]
    stats_all = summed[pool_rows + conv_rows :].reshape(stats_sum.shape)
    grad_conv_b = stats_all[0, :width]
    grad_pool_b = stats_all[0, width:]
    loss_sum = stats_all[1, 0]
    return (embedding, loss_sum, grad_pool_w, grad_pool_b, grad_conv_w, grad_conv_b)


def solution(mesh):
    owners, groups = mesh.devices.shape
    cores = 2
    rows_y = 4 if owners % (cores * 4) == 0 else 1
    fine = Mesh(
        mesh.devices.reshape(owners // (cores * rows_y), rows_y, cores, groups),
        OWNER + ("neg",),
    )
    spread = OWNER + ("neg",)
    return jax.shard_map(
        local,
        mesh=fine,
        in_specs=(
            P(spread, None),
            P(spread, None),
            P(spread),
            P(spread),
            P(spread, None),
            P(OWNER, None),
            P(),
            P(),
            P(),
            P(),
        ),
        out_specs=(P(spread, None), P(), P(OWNER, None), P(), P(OWNER, None), P()),
        check_vma=False,
    )
```

```python
import jax
import jax.numpy as jnp
from jax import lax
from jax.sharding import Mesh, PartitionSpec as P

margin_value = 0.5
OWNER = ("oz", "oy", "oc")


def silu_slope(values):
    sig = jax.nn.sigmoid(values)
    return sig * (1.0 + values * (1.0 - sig))


def forward(pooled, self_rows, w_pool, b_pool, w_conv, b_conv):
    pooled_b = pooled.astype(jnp.bfloat16)
    pre_pool = jnp.dot(pooled_b, w_pool, preferred_element_type=jnp.float32) + b_pool
    neighbour = jax.nn.silu(pre_pool).astype(jnp.bfloat16)
    joined = jnp.concatenate([self_rows, neighbour], axis=1)
    pre_conv = jnp.dot(joined, w_conv, preferred_element_type=jnp.float32) + b_conv
    hidden = jax.nn.silu(pre_conv)
    inverse = lax.rsqrt(jnp.sum(hidden * hidden, axis=1, keepdims=True) + 1e-05)
    embedding = hidden * inverse
    return (pooled_b, pre_pool, joined, pre_conv, inverse, embedding)


def margin_terms(neg_scores, pos_scores, loss_scale):
    margins = neg_scores - pos_scores[:, None] + margin_value
    loss_part = jnp.sum(jax.nn.softplus(margins)) * loss_scale
    slope_b = jax.nn.sigmoid(margins).astype(jnp.bfloat16)
    slope_total = jnp.sum(slope_b.astype(jnp.float32), axis=1, keepdims=True)
    return (loss_part, slope_b, slope_total)


def backward_factors(d_embed, embedding, inverse, pre_conv, pre_pool, w_conv, grad_scale):
    width = embedding.shape[1]
    radial = jnp.sum(d_embed * embedding, axis=1, keepdims=True)
    d_pre_conv = silu_slope(pre_conv) * inverse * (d_embed - embedding * radial) * grad_scale
    d_conv_b = d_pre_conv.astype(jnp.bfloat16)
    grad_conv_b = jnp.sum(d_pre_conv, axis=0)
    d_neighbour = lax.dot_general(
        d_conv_b, w_conv[width:], (((1,), (1,)), ((), ())), preferred_element_type=jnp.float32
    )
    d_pre_pool = silu_slope(pre_pool) * d_neighbour
    d_pool_b = d_pre_pool.astype(jnp.bfloat16)
    grad_pool_b = jnp.sum(d_pre_pool, axis=0)
    return (d_conv_b, d_pool_b, grad_pool_b, grad_conv_b)


def weight_grads(joined, pooled_b, d_conv_b, d_pool_b, stats):
    owners = lax.axis_size(OWNER)
    queries = joined.shape[0]
    conv_rows = joined.shape[1] // owners
    pool_rows = pooled_b.shape[1] // owners
    left = jnp.concatenate(
        [
            joined.reshape(queries, owners, conv_rows).transpose(1, 0, 2),
            pooled_b.reshape(queries, owners, pool_rows).transpose(1, 0, 2),
        ],
        axis=2,
    )
    left = lax.all_to_all(left, OWNER, split_axis=0, concat_axis=0, tiled=True)
    left = left.reshape(owners * queries, conv_rows + pool_rows)
    stats_hi = stats.astype(jnp.bfloat16)
    stats_lo = (stats - stats_hi.astype(jnp.float32)).astype(jnp.bfloat16)
    payload = jnp.concatenate([d_conv_b, d_pool_b], axis=1)
    payload = jnp.concatenate([payload, stats_hi, stats_lo], axis=0)
    gathered = lax.all_gather(payload, OWNER[2], axis=0)
    gathered = lax.all_gather(gathered, OWNER[:2], axis=0)
    gathered = gathered.reshape((owners,) + payload.shape)
    right = gathered[:, :queries].reshape(owners * queries, payload.shape[1])
    stat_rows = stats.shape[0]
    stats_sum = jnp.sum(
        gathered[:, queries : queries + stat_rows].astype(jnp.float32)
        + gathered[:, queries + stat_rows :].astype(jnp.float32),
        axis=0,
    )
    contract_rows = (((0,), (0,)), ((), ()))
    conv_width = d_conv_b.shape[1]
    conv_part = lax.dot_general(
        left[:, :conv_rows], right[:, :conv_width], contract_rows,
        preferred_element_type=jnp.float32,
    )
    pool_part = lax.dot_general(
        left[:, conv_rows:], right[:, conv_width:], contract_rows,
        preferred_element_type=jnp.float32,
    )
    return pool_part, conv_part, stats_sum


def pair_sum(values, groups):
    step = 1
    while step < groups:
        partner = lax.ppermute(values, "neg", [(i, i ^ step) for i in range(groups)])
        values = values + partner
        step *= 2
    return values


def bucket(page_list, owners, rows_per, capacity):
    count = page_list.shape[0]
    owner_of = page_list // rows_per
    local_row = page_list - owner_of * rows_per
    one_hot = (owner_of[:, None] == jnp.arange(owners, dtype=jnp.int32)[None, :]).astype(jnp.bfloat16)
    positions = jnp.arange(count, dtype=jnp.int32)
    earlier = (positions[:, None] > positions[None, :]).astype(jnp.bfloat16)
    before = jnp.dot(earlier, one_hot, preferred_element_type=jnp.float32)
    slot_of = jnp.sum(before * one_hot.astype(jnp.float32), axis=1).astype(jnp.int32)
    flat = owner_of * capacity + slot_of
    select = (flat[:, None] == jnp.arange(owners * capacity, dtype=jnp.int32)[None, :]).astype(jnp.bfloat16)
    parts = jnp.stack([local_row // 64, local_row % 64]).astype(jnp.bfloat16)
    placed = jnp.dot(parts, select, preferred_element_type=jnp.float32).astype(jnp.int32)
    requests = (placed[0] * 64 + placed[1]).reshape(owners, capacity)
    return (owner_of, slot_of, requests)


def local(nbr_ids, visit_counts, self_ids, pos_ids, neg_ids, table, w_pool, b_pool, w_conv, b_conv):
    owners = lax.axis_size(OWNER)
    groups = lax.axis_size("neg")
    rows_per = table.shape[0]
    width = table.shape[1]
    queries, fan_count = nbr_ids.shape
    neg_count = neg_ids.shape[1]
    counts_f = visit_counts.astype(jnp.float32)
    weights = counts_f / jnp.sum(counts_f, axis=1, keepdims=True)
    flat_ids = nbr_ids.reshape(-1)
    capacity = 2 * (flat_ids.shape[0] // owners) + 4
    page_cap = 2 * (queries * (neg_count + 2) // owners) + 4
    capacity = -(-capacity // 8) * 8
    page_cap = -(-page_cap // 8) * 8
    total_queries = queries * owners * groups
    grad_scale = 1.0 / neg_count
    loss_scale = 1.0 / (total_queries * neg_count)
    owner_of, slot_of, requests = bucket(flat_ids, owners, rows_per, capacity)
    page_list = jnp.concatenate([self_ids, pos_ids, neg_ids.reshape(-1)])
    page_owner, page_slot, page_requests = bucket(page_list, owners, rows_per, page_cap)
    slots = capacity + page_cap
    all_requests = jnp.concatenate([requests, page_requests], axis=1)
    served = lax.all_to_all(all_requests, OWNER, split_axis=0, concat_axis=0, tiled=True)
    returned = lax.all_to_all(
        table[served.reshape(-1)].reshape(owners, slots, width),
        OWNER, split_axis=0, concat_axis=0, tiled=True,
    )
    nbr_rows = returned[:, :capacity].reshape(owners * capacity, width)
    page_rows = returned[:, capacity:].reshape(owners * page_cap, width)
    nbr_flat = (owner_of * capacity + slot_of).reshape(queries, fan_count)
    nbr_slots = jnp.arange(owners * capacity, dtype=jnp.int32)
    pool_weights = jnp.sum(
        jnp.where(nbr_flat[:, :, None] == nbr_slots[None, None, :], weights[:, :, None], 0.0), axis=1
    )
    pooled = jnp.dot(
        pool_weights, nbr_rows.astype(jnp.float32), precision=lax.Precision.HIGHEST,
        preferred_element_type=jnp.float32,
    )
    page_flat = page_owner * page_cap + page_slot
    page_slots = jnp.arange(owners * page_cap, dtype=jnp.int32)
    self_flat = page_flat[:queries]
    pos_flat = page_flat[queries : 2 * queries]
    neg_flat = page_flat[2 * queries :].reshape(queries, neg_count)
    pick = (jnp.stack([self_flat, pos_flat])[:, :, None] == page_slots[None, None, :]).astype(jnp.bfloat16)
    picked = jnp.einsum("aqs,se->aqe", pick, page_rows, preferred_element_type=jnp.float32)
    self_rows = picked[0].astype(jnp.bfloat16)
    pos_rows = picked[1].astype(jnp.bfloat16)
    pooled_b, pre_pool, joined, pre_conv, inverse, embedding = forward(
        pooled, self_rows, w_pool, b_pool, w_conv, b_conv
    )
    embed_b = embedding.astype(jnp.bfloat16)
    slot_scores = lax.dot_general(
        embed_b, page_rows, (((1,), (1,)), ((), ())), preferred_element_type=jnp.float32
    )
    neg_scores = jnp.take_along_axis(slot_scores, neg_flat, axis=1)
    pos_scores = jnp.einsum("qe,qe->q", embed_b, pos_rows, preferred_element_type=jnp.float32)
    loss_part, slope_b, slope_total = margin_terms(neg_scores, pos_scores, loss_scale)
    slope_slots = jnp.sum(
        jnp.where(
            neg_flat[:, :, None] == page_slots[None, None, :],
            slope_b.astype(jnp.float32)[:, :, None],
            0.0,
        ),
        axis=1,
    ).astype(jnp.bfloat16)
    d_embed = jnp.dot(
        slope_slots, page_rows, preferred_element_type=jnp.float32
    ) - slope_total * pos_rows.astype(jnp.float32)
    d_conv_b, d_pool_b, pool_bgrad, conv_bgrad = backward_factors(
        d_embed, embedding, inverse, pre_conv, pre_pool, w_conv, grad_scale
    )
    loss_row = jnp.zeros((2 * width,), jnp.float32).at[0].set(loss_part)
    stats = jnp.stack([jnp.concatenate([conv_bgrad, pool_bgrad]), loss_row])
    pool_part, conv_part, stats_sum = weight_grads(joined, pooled_b, d_conv_b, d_pool_b, stats)
    pool_rows = pool_part.shape[0]
    conv_rows = conv_part.shape[0]
    summed = pair_sum(
        jnp.concatenate([pool_part, conv_part, stats_sum.reshape(-1, width)], axis=0), groups
    )
    grad_pool_w = summed[:pool_rows]
    grad_conv_w = summed[pool_rows : pool_rows + conv_rows]
    stats_all = summed[pool_rows + conv_rows :].reshape(stats_sum.shape)
    grad_conv_b = stats_all[0, :width]
    grad_pool_b = stats_all[0, width:]
    loss_sum = stats_all[1, 0]
    return (embedding, loss_sum, grad_pool_w, grad_pool_b, grad_conv_w, grad_conv_b)


def solution(mesh):
    owners, groups = mesh.devices.shape
    cores = 2
    rows_y = 4 if owners % (cores * 4) == 0 else 1
    fine = Mesh(
        mesh.devices.reshape(owners // (cores * rows_y), rows_y, cores, groups),
        OWNER + ("neg",),
    )
    spread = OWNER + ("neg",)
    return jax.shard_map(
        local,
        mesh=fine,
        in_specs=(
            P(spread, None),
            P(spread, None),
            P(spread),
            P(spread),
            P(spread, None),
            P(OWNER, None),
            P(),
            P(),
            P(),
            P(),
        ),
        out_specs=(P(spread, None), P(), P(OWNER, None), P(), P(OWNER, None), P()),
        check_vma=False,
    )
```

```python
import jax
import jax.numpy as jnp
from jax import lax
from jax.sharding import Mesh, PartitionSpec as P

margin_value = 0.5
OWNER = ("oz", "oy", "oc")


def silu_slope(values):
    sig = jax.nn.sigmoid(values)
    return sig * (1.0 + values * (1.0 - sig))


def forward(pooled, self_rows, w_pool, b_pool, w_conv, b_conv):
    pooled_b = pooled.astype(jnp.bfloat16)
    pre_pool = jnp.dot(pooled_b, w_pool, preferred_element_type=jnp.float32) + b_pool
    neighbour = jax.nn.silu(pre_pool).astype(jnp.bfloat16)
    joined = jnp.concatenate([self_rows, neighbour], axis=1)
    pre_conv = jnp.dot(joined, w_conv, preferred_element_type=jnp.float32) + b_conv
    hidden = jax.nn.silu(pre_conv)
    inverse = lax.rsqrt(jnp.sum(hidden * hidden, axis=1, keepdims=True) + 1e-05)
    embedding = hidden * inverse
    return (pooled_b, pre_pool, joined, pre_conv, inverse, embedding)


def margin_terms(neg_scores, pos_scores, loss_scale):
    margins = neg_scores - pos_scores[:, None] + margin_value
    loss_part = jnp.sum(jax.nn.softplus(margins)) * loss_scale
    slope_b = jax.nn.sigmoid(margins).astype(jnp.bfloat16)
    slope_total = jnp.sum(slope_b.astype(jnp.float32), axis=1, keepdims=True)
    return (loss_part, slope_b, slope_total)


def backward_factors(d_embed, embedding, inverse, pre_conv, pre_pool, w_conv, grad_scale):
    width = embedding.shape[1]
    radial = jnp.sum(d_embed * embedding, axis=1, keepdims=True)
    d_pre_conv = silu_slope(pre_conv) * inverse * (d_embed - embedding * radial) * grad_scale
    d_conv_b = d_pre_conv.astype(jnp.bfloat16)
    grad_conv_b = jnp.sum(d_pre_conv, axis=0)
    d_neighbour = lax.dot_general(
        d_conv_b, w_conv[width:], (((1,), (1,)), ((), ())), preferred_element_type=jnp.float32
    )
    d_pre_pool = silu_slope(pre_pool) * d_neighbour
    d_pool_b = d_pre_pool.astype(jnp.bfloat16)
    grad_pool_b = jnp.sum(d_pre_pool, axis=0)
    return (d_conv_b, d_pool_b, grad_pool_b, grad_conv_b)


def weight_grads(joined, pooled_b, d_conv_b, d_pool_b, stats):
    owners = lax.axis_size(OWNER)
    queries = joined.shape[0]
    conv_rows = joined.shape[1] // owners
    pool_rows = pooled_b.shape[1] // owners
    left = jnp.concatenate(
        [
            joined.reshape(queries, owners, conv_rows).transpose(1, 0, 2),
            pooled_b.reshape(queries, owners, pool_rows).transpose(1, 0, 2),
        ],
        axis=2,
    )
    left = lax.all_to_all(left, OWNER, split_axis=0, concat_axis=0, tiled=True)
    stats_hi = stats.astype(jnp.bfloat16)
    stats_lo = (stats - stats_hi.astype(jnp.float32)).astype(jnp.bfloat16)
    payload = jnp.concatenate([d_conv_b, d_pool_b], axis=1)
    payload = jnp.concatenate([payload, stats_hi, stats_lo], axis=0)
    gathered = lax.all_gather(payload, OWNER[2], axis=0)
    gathered = lax.all_gather(gathered, OWNER[1], axis=0)
    ring = ring_gather(gathered, OWNER[0], lax.axis_size(OWNER[0]))
    here = lax.axis_index(OWNER[0])
    left = jnp.roll(left.reshape((ring.shape[0], -1) + left.shape[1:]), -here, axis=0)
    left = left.reshape(owners * queries, conv_rows + pool_rows)
    right = ring[:, :, :, :queries].reshape(owners * queries, payload.shape[1])
    stat_rows = stats.shape[0]
    stat_parts = jnp.roll(ring[:, :, :, queries:], here, axis=0).astype(jnp.float32)
    stats_sum = jnp.sum(
        stat_parts[:, :, :, :stat_rows] + stat_parts[:, :, :, stat_rows:], axis=(0, 1, 2)
    )
    contract_rows = (((0,), (0,)), ((), ()))
    conv_width = d_conv_b.shape[1]
    conv_part = lax.dot_general(
        left[:, :conv_rows], right[:, :conv_width], contract_rows,
        preferred_element_type=jnp.float32,
    )
    pool_part = lax.dot_general(
        left[:, conv_rows:], right[:, conv_width:], contract_rows,
        preferred_element_type=jnp.float32,
    )
    return pool_part, conv_part, stats_sum


def ring_gather(block, axis, size):
    ahead, behind = [], []
    forward_part, backward_part = block, block
    for step in range(1, size // 2 + 1):
        forward_part = lax.ppermute(forward_part, axis, [(i, (i + 1) % size) for i in range(size)])
        behind.append(forward_part)
        if 2 * step < size:
            backward_part = lax.ppermute(backward_part, axis, [(i, (i - 1) % size) for i in range(size)])
            ahead.append(backward_part)
    return jnp.stack([block] + ahead + behind[::-1])


def pair_sum(values, groups):
    step = 1
    while step < groups:
        partner = lax.ppermute(values, "neg", [(i, i ^ step) for i in range(groups)])
        values = values + partner
        step *= 2
    return values


def bucket(page_list, owners, rows_per, capacity):
    count = page_list.shape[0]
    owner_of = page_list // rows_per
    local_row = page_list - owner_of * rows_per
    one_hot = (owner_of[:, None] == jnp.arange(owners, dtype=jnp.int32)[None, :]).astype(jnp.bfloat16)
    positions = jnp.arange(count, dtype=jnp.int32)
    earlier = (positions[:, None] > positions[None, :]).astype(jnp.bfloat16)
    before = jnp.dot(earlier, one_hot, preferred_element_type=jnp.float32)
    slot_of = jnp.sum(before * one_hot.astype(jnp.float32), axis=1).astype(jnp.int32)
    flat = owner_of * capacity + slot_of
    select = (flat[:, None] == jnp.arange(owners * capacity, dtype=jnp.int32)[None, :]).astype(jnp.bfloat16)
    parts = jnp.stack([local_row // 64, local_row % 64]).astype(jnp.bfloat16)
    placed = jnp.dot(parts, select, preferred_element_type=jnp.float32).astype(jnp.int32)
    requests = (placed[0] * 64 + placed[1]).reshape(owners, capacity)
    return (owner_of, slot_of, requests)


def local(nbr_ids, visit_counts, self_ids, pos_ids, neg_ids, table, w_pool, b_pool, w_conv, b_conv):
    owners = lax.axis_size(OWNER)
    groups = lax.axis_size("neg")
    rows_per = table.shape[0]
    width = table.shape[1]
    queries, fan_count = nbr_ids.shape
    neg_count = neg_ids.shape[1]
    counts_f = visit_counts.astype(jnp.float32)
    weights = counts_f / jnp.sum(counts_f, axis=1, keepdims=True)
    flat_ids = nbr_ids.reshape(-1)
    capacity = 2 * (flat_ids.shape[0] // owners) + 4
    page_cap = 2 * (queries * (neg_count + 2) // owners) + 4
    capacity = -(-capacity // 8) * 8
    page_cap = -(-page_cap // 8) * 8
    total_queries = queries * owners * groups
    grad_scale = 1.0 / neg_count
    loss_scale = 1.0 / (total_queries * neg_count)
    owner_of, slot_of, requests = bucket(flat_ids, owners, rows_per, capacity)
    page_list = jnp.concatenate([self_ids, pos_ids, neg_ids.reshape(-1)])
    page_owner, page_slot, page_requests = bucket(page_list, owners, rows_per, page_cap)
    slots = capacity + page_cap
    all_requests = jnp.concatenate([requests, page_requests], axis=1)
    served = lax.all_to_all(all_requests, OWNER, split_axis=0, concat_axis=0, tiled=True)
    returned = lax.all_to_all(
        table[served.reshape(-1)].reshape(owners, slots, width),
        OWNER, split_axis=0, concat_axis=0, tiled=True,
    )
    nbr_rows = returned[:, :capacity].reshape(owners * capacity, width)
    page_rows = returned[:, capacity:].reshape(owners * page_cap, width)
    nbr_flat = (owner_of * capacity + slot_of).reshape(queries, fan_count)
    nbr_slots = jnp.arange(owners * capacity, dtype=jnp.int32)
    pool_weights = jnp.sum(
        jnp.where(nbr_flat[:, :, None] == nbr_slots[None, None, :], weights[:, :, None], 0.0), axis=1
    )
    pooled = jnp.dot(
        pool_weights, nbr_rows.astype(jnp.float32), precision=lax.Precision.HIGHEST,
        preferred_element_type=jnp.float32,
    )
    page_flat = page_owner * page_cap + page_slot
    page_slots = jnp.arange(owners * page_cap, dtype=jnp.int32)
    self_flat = page_flat[:queries]
    pos_flat = page_flat[queries : 2 * queries]
    neg_flat = page_flat[2 * queries :].reshape(queries, neg_count)
    pick = (jnp.stack([self_flat, pos_flat])[:, :, None] == page_slots[None, None, :]).astype(jnp.bfloat16)
    picked = jnp.einsum("aqs,se->aqe", pick, page_rows, preferred_element_type=jnp.float32)
    self_rows = picked[0].astype(jnp.bfloat16)
    pos_rows = picked[1].astype(jnp.bfloat16)
    pooled_b, pre_pool, joined, pre_conv, inverse, embedding = forward(
        pooled, self_rows, w_pool, b_pool, w_conv, b_conv
    )
    embed_b = embedding.astype(jnp.bfloat16)
    slot_scores = lax.dot_general(
        embed_b, page_rows, (((1,), (1,)), ((), ())), preferred_element_type=jnp.float32
    )
    neg_scores = jnp.take_along_axis(slot_scores, neg_flat, axis=1)
    pos_scores = jnp.einsum("qe,qe->q", embed_b, pos_rows, preferred_element_type=jnp.float32)
    loss_part, slope_b, slope_total = margin_terms(neg_scores, pos_scores, loss_scale)
    slope_slots = jnp.sum(
        jnp.where(
            neg_flat[:, :, None] == page_slots[None, None, :],
            slope_b.astype(jnp.float32)[:, :, None],
            0.0,
        ),
        axis=1,
    ).astype(jnp.bfloat16)
    d_embed = jnp.dot(
        slope_slots, page_rows, preferred_element_type=jnp.float32
    ) - slope_total * pos_rows.astype(jnp.float32)
    d_conv_b, d_pool_b, pool_bgrad, conv_bgrad = backward_factors(
        d_embed, embedding, inverse, pre_conv, pre_pool, w_conv, grad_scale
    )
    loss_row = jnp.zeros((2 * width,), jnp.float32).at[0].set(loss_part)
    stats = jnp.stack([jnp.concatenate([conv_bgrad, pool_bgrad]), loss_row])
    pool_part, conv_part, stats_sum = weight_grads(joined, pooled_b, d_conv_b, d_pool_b, stats)
    pool_rows = pool_part.shape[0]
    conv_rows = conv_part.shape[0]
    summed = pair_sum(
        jnp.concatenate([pool_part, conv_part, stats_sum.reshape(-1, width)], axis=0), groups
    )
    grad_pool_w = summed[:pool_rows]
    grad_conv_w = summed[pool_rows : pool_rows + conv_rows]
    stats_all = summed[pool_rows + conv_rows :].reshape(stats_sum.shape)
    grad_conv_b = stats_all[0, :width]
    grad_pool_b = stats_all[0, width:]
    loss_sum = stats_all[1, 0]
    return (embedding, loss_sum, grad_pool_w, grad_pool_b, grad_conv_w, grad_conv_b)


def solution(mesh):
    owners, groups = mesh.devices.shape
    cores = 2
    rows_y = 4 if owners % (cores * 4) == 0 else 1
    fine = Mesh(
        mesh.devices.reshape(owners // (cores * rows_y), rows_y, cores, groups),
        OWNER + ("neg",),
    )
    spread = OWNER + ("neg",)
    return jax.shard_map(
        local,
        mesh=fine,
        in_specs=(
            P(spread, None),
            P(spread, None),
            P(spread),
            P(spread),
            P(spread, None),
            P(OWNER, None),
            P(),
            P(),
            P(),
            P(),
        ),
        out_specs=(P(spread, None), P(), P(OWNER, None), P(), P(OWNER, None), P()),
        check_vma=False,
    )
```

```python
import jax
import jax.numpy as jnp
from jax import lax
from jax.sharding import Mesh, PartitionSpec as P

margin_value = 0.5
OWNER = ("oz", "oy", "oc")


def silu_slope(values):
    sig = jax.nn.sigmoid(values)
    return sig * (1.0 + values * (1.0 - sig))


def forward(pooled, self_rows, w_pool, b_pool, w_conv, b_conv):
    pooled_b = pooled.astype(jnp.bfloat16)
    pre_pool = jnp.dot(pooled_b, w_pool, preferred_element_type=jnp.float32) + b_pool
    neighbour = jax.nn.silu(pre_pool).astype(jnp.bfloat16)
    joined = jnp.concatenate([self_rows, neighbour], axis=1)
    pre_conv = jnp.dot(joined, w_conv, preferred_element_type=jnp.float32) + b_conv
    hidden = jax.nn.silu(pre_conv)
    inverse = lax.rsqrt(jnp.sum(hidden * hidden, axis=1, keepdims=True) + 1e-05)
    embedding = hidden * inverse
    return (pooled_b, pre_pool, joined, pre_conv, inverse, embedding)


def margin_terms(neg_scores, pos_scores, loss_scale):
    margins = neg_scores - pos_scores[:, None] + margin_value
    loss_part = jnp.sum(jax.nn.softplus(margins)) * loss_scale
    slope_b = jax.nn.sigmoid(margins).astype(jnp.bfloat16)
    slope_total = jnp.sum(slope_b.astype(jnp.float32), axis=1, keepdims=True)
    return (loss_part, slope_b, slope_total)


def backward_factors(d_embed, embedding, inverse, pre_conv, pre_pool, w_conv, grad_scale):
    width = embedding.shape[1]
    radial = jnp.sum(d_embed * embedding, axis=1, keepdims=True)
    d_pre_conv = silu_slope(pre_conv) * inverse * (d_embed - embedding * radial) * grad_scale
    d_conv_b = d_pre_conv.astype(jnp.bfloat16)
    grad_conv_b = jnp.sum(d_pre_conv, axis=0)
    d_neighbour = lax.dot_general(
        d_conv_b, w_conv[width:], (((1,), (1,)), ((), ())), preferred_element_type=jnp.float32
    )
    d_pre_pool = silu_slope(pre_pool) * d_neighbour
    d_pool_b = d_pre_pool.astype(jnp.bfloat16)
    grad_pool_b = jnp.sum(d_pre_pool, axis=0)
    return (d_conv_b, d_pool_b, grad_pool_b, grad_conv_b)


def weight_grads(joined, pooled_b, d_conv_b, d_pool_b, stats):
    owners = lax.axis_size(OWNER)
    queries = joined.shape[0]
    conv_rows = joined.shape[1] // owners
    pool_rows = pooled_b.shape[1] // owners
    left = jnp.concatenate(
        [
            joined.reshape(queries, owners, conv_rows).transpose(1, 0, 2),
            pooled_b.reshape(queries, owners, pool_rows).transpose(1, 0, 2),
        ],
        axis=2,
    )
    left = lax.all_to_all(left, OWNER, split_axis=0, concat_axis=0, tiled=True)
    stats_hi = stats.astype(jnp.bfloat16)
    stats_lo = (stats - stats_hi.astype(jnp.float32)).astype(jnp.bfloat16)
    payload = jnp.concatenate([d_conv_b, d_pool_b], axis=1)
    payload = jnp.concatenate([payload, stats_hi, stats_lo], axis=0)
    gathered = lax.all_gather(payload, OWNER[2], axis=0)
    gathered = lax.all_gather(gathered, OWNER[1], axis=0)
    ring = ring_gather(gathered, OWNER[0], lax.axis_size(OWNER[0]))
    here = lax.axis_index(OWNER[0])
    left = jnp.roll(left.reshape((ring.shape[0], -1) + left.shape[1:]), -here, axis=0)
    left = left.reshape(owners * queries, conv_rows + pool_rows)
    right = ring[:, :, :, :queries].reshape(owners * queries, payload.shape[1])
    stat_rows = stats.shape[0]
    stat_parts = jnp.roll(ring[:, :, :, queries:], here, axis=0).astype(jnp.float32)
    stats_sum = jnp.sum(
        stat_parts[:, :, :, :stat_rows] + stat_parts[:, :, :, stat_rows:], axis=(0, 1, 2)
    )
    contract_rows = (((0,), (0,)), ((), ()))
    conv_width = d_conv_b.shape[1]
    conv_part = lax.dot_general(
        left[:, :conv_rows], right[:, :conv_width], contract_rows,
        preferred_element_type=jnp.float32,
    )
    pool_part = lax.dot_general(
        left[:, conv_rows:], right[:, conv_width:], contract_rows,
        preferred_element_type=jnp.float32,
    )
    return pool_part, conv_part, stats_sum


def ring_gather(block, axis, size):
    ahead, behind = [], []
    forward_part, backward_part = block, block
    for step in range(1, size // 2 + 1):
        forward_part = lax.ppermute(forward_part, axis, [(i, (i + 1) % size) for i in range(size)])
        behind.append(forward_part)
        if 2 * step < size:
            backward_part = lax.ppermute(backward_part, axis, [(i, (i - 1) % size) for i in range(size)])
            ahead.append(backward_part)
    return jnp.stack([block] + ahead + behind[::-1])


def pair_sum(values, groups):
    step = 1
    while step < groups:
        partner = lax.ppermute(values, "neg", [(i, i ^ step) for i in range(groups)])
        values = values + partner
        step *= 2
    return values


def bucket(page_list, owners, rows_per, capacity):
    count = page_list.shape[0]
    owner_of = page_list // rows_per
    local_row = page_list - owner_of * rows_per
    one_hot = (owner_of[:, None] == jnp.arange(owners, dtype=jnp.int32)[None, :]).astype(jnp.bfloat16)
    positions = jnp.arange(count, dtype=jnp.int32)
    earlier = (positions[:, None] > positions[None, :]).astype(jnp.bfloat16)
    before = jnp.dot(earlier, one_hot, preferred_element_type=jnp.float32)
    slot_of = jnp.sum(before * one_hot.astype(jnp.float32), axis=1).astype(jnp.int32)
    flat = owner_of * capacity + slot_of
    select = (flat[:, None] == jnp.arange(owners * capacity, dtype=jnp.int32)[None, :]).astype(jnp.bfloat16)
    parts = jnp.stack([local_row // 64, local_row % 64]).astype(jnp.bfloat16)
    placed = jnp.dot(parts, select, preferred_element_type=jnp.float32).astype(jnp.int32)
    requests = (placed[0] * 64 + placed[1]).reshape(owners, capacity)
    return (owner_of, slot_of, requests)


def local(nbr_ids, visit_counts, self_ids, pos_ids, neg_ids, table, w_pool, b_pool, w_conv, b_conv):
    owners = lax.axis_size(OWNER)
    groups = lax.axis_size("neg")
    rows_per = table.shape[0]
    width = table.shape[1]
    queries, fan_count = nbr_ids.shape
    neg_count = neg_ids.shape[1]
    counts_f = visit_counts.astype(jnp.float32)
    weights = counts_f / jnp.sum(counts_f, axis=1, keepdims=True)
    flat_ids = nbr_ids.reshape(-1)
    capacity = 2 * (flat_ids.shape[0] // owners) + 4
    page_cap = 2 * (queries * (neg_count + 2) // owners) + 4
    capacity = -(-capacity // 8) * 8
    page_cap = -(-page_cap // 8) * 8
    total_queries = queries * owners * groups
    grad_scale = 1.0 / neg_count
    loss_scale = 1.0 / (total_queries * neg_count)
    owner_of, slot_of, requests = bucket(flat_ids, owners, rows_per, capacity)
    page_list = jnp.concatenate([self_ids, pos_ids, neg_ids.reshape(-1)])
    page_owner, page_slot, page_requests = bucket(page_list, owners, rows_per, page_cap)
    slots = capacity + page_cap
    all_requests = jnp.concatenate([requests, page_requests], axis=1)
    served = lax.all_to_all(all_requests, OWNER, split_axis=0, concat_axis=0, tiled=True)
    nbr_rows = lax.all_to_all(
        table[served[:, :capacity].reshape(-1)].reshape(owners, capacity, width),
        OWNER, split_axis=0, concat_axis=0, tiled=True,
    ).reshape(owners * capacity, width)
    page_rows = lax.all_to_all(
        table[served[:, capacity:].reshape(-1)].reshape(owners, page_cap, width),
        OWNER, split_axis=0, concat_axis=0, tiled=True,
    ).reshape(owners * page_cap, width)
    nbr_flat = (owner_of * capacity + slot_of).reshape(queries, fan_count)
    nbr_slots = jnp.arange(owners * capacity, dtype=jnp.int32)
    pool_weights = jnp.sum(
        jnp.where(nbr_flat[:, :, None] == nbr_slots[None, None, :], weights[:, :, None], 0.0), axis=1
    )
    pooled = jnp.dot(
        pool_weights, nbr_rows.astype(jnp.float32), precision=lax.Precision.HIGHEST,
        preferred_element_type=jnp.float32,
    )
    page_flat = page_owner * page_cap + page_slot
    page_slots = jnp.arange(owners * page_cap, dtype=jnp.int32)
    self_flat = page_flat[:queries]
    pos_flat = page_flat[queries : 2 * queries]
    neg_flat = page_flat[2 * queries :].reshape(queries, neg_count)
    pick = (jnp.stack([self_flat, pos_flat])[:, :, None] == page_slots[None, None, :]).astype(jnp.bfloat16)
    picked = jnp.einsum("aqs,se->aqe", pick, page_rows, preferred_element_type=jnp.float32)
    self_rows = picked[0].astype(jnp.bfloat16)
    pos_rows = picked[1].astype(jnp.bfloat16)
    pooled_b, pre_pool, joined, pre_conv, inverse, embedding = forward(
        pooled, self_rows, w_pool, b_pool, w_conv, b_conv
    )
    embed_b = embedding.astype(jnp.bfloat16)
    slot_scores = lax.dot_general(
        embed_b, page_rows, (((1,), (1,)), ((), ())), preferred_element_type=jnp.float32
    )
    neg_scores = jnp.take_along_axis(slot_scores, neg_flat, axis=1)
    pos_scores = jnp.einsum("qe,qe->q", embed_b, pos_rows, preferred_element_type=jnp.float32)
    loss_part, slope_b, slope_total = margin_terms(neg_scores, pos_scores, loss_scale)
    slope_slots = jnp.sum(
        jnp.where(
            neg_flat[:, :, None] == page_slots[None, None, :],
            slope_b.astype(jnp.float32)[:, :, None],
            0.0,
        ),
        axis=1,
    ).astype(jnp.bfloat16)
    d_embed = jnp.dot(
        slope_slots, page_rows, preferred_element_type=jnp.float32
    ) - slope_total * pos_rows.astype(jnp.float32)
    d_conv_b, d_pool_b, pool_bgrad, conv_bgrad = backward_factors(
        d_embed, embedding, inverse, pre_conv, pre_pool, w_conv, grad_scale
    )
    loss_row = jnp.zeros((2 * width,), jnp.float32).at[0].set(loss_part)
    stats = jnp.stack([jnp.concatenate([conv_bgrad, pool_bgrad]), loss_row])
    pool_part, conv_part, stats_sum = weight_grads(joined, pooled_b, d_conv_b, d_pool_b, stats)
    pool_rows = pool_part.shape[0]
    conv_rows = conv_part.shape[0]
    summed = pair_sum(
        jnp.concatenate([pool_part, conv_part, stats_sum.reshape(-1, width)], axis=0), groups
    )
    grad_pool_w = summed[:pool_rows]
    grad_conv_w = summed[pool_rows : pool_rows + conv_rows]
    stats_all = summed[pool_rows + conv_rows :].reshape(stats_sum.shape)
    grad_conv_b = stats_all[0, :width]
    grad_pool_b = stats_all[0, width:]
    loss_sum = stats_all[1, 0]
    return (embedding, loss_sum, grad_pool_w, grad_pool_b, grad_conv_w, grad_conv_b)


def solution(mesh):
    owners, groups = mesh.devices.shape
    cores = 2
    rows_y = 4 if owners % (cores * 4) == 0 else 1
    fine = Mesh(
        mesh.devices.reshape(owners // (cores * rows_y), rows_y, cores, groups),
        OWNER + ("neg",),
    )
    spread = OWNER + ("neg",)
    return jax.shard_map(
        local,
        mesh=fine,
        in_specs=(
            P(spread, None),
            P(spread, None),
            P(spread),
            P(spread),
            P(spread, None),
            P(OWNER, None),
            P(),
            P(),
            P(),
            P(),
        ),
        out_specs=(P(spread, None), P(), P(OWNER, None), P(), P(OWNER, None), P()),
        check_vma=False,
    )
```

```python
import jax
import jax.numpy as jnp
from jax import lax
from jax.sharding import Mesh, PartitionSpec as P

margin_value = 0.5
OWNER = ("oz", "oy", "oc")


def silu_slope(values):
    sig = jax.nn.sigmoid(values)
    return sig * (1.0 + values * (1.0 - sig))


def forward(pooled, self_rows, w_pool, b_pool, w_conv, b_conv):
    pooled_b = pooled.astype(jnp.bfloat16)
    pre_pool = jnp.dot(pooled_b, w_pool, preferred_element_type=jnp.float32) + b_pool
    neighbour = jax.nn.silu(pre_pool).astype(jnp.bfloat16)
    joined = jnp.concatenate([self_rows, neighbour], axis=1)
    pre_conv = jnp.dot(joined, w_conv, preferred_element_type=jnp.float32) + b_conv
    hidden = jax.nn.silu(pre_conv)
    inverse = lax.rsqrt(jnp.sum(hidden * hidden, axis=1, keepdims=True) + 1e-05)
    embedding = hidden * inverse
    return (pooled_b, pre_pool, joined, pre_conv, inverse, embedding)


def margin_terms(neg_scores, pos_scores, loss_scale):
    margins = neg_scores - pos_scores[:, None] + margin_value
    loss_part = jnp.sum(jax.nn.softplus(margins)) * loss_scale
    slope_b = jax.nn.sigmoid(margins).astype(jnp.bfloat16)
    slope_total = jnp.sum(slope_b.astype(jnp.float32), axis=1, keepdims=True)
    return (loss_part, slope_b, slope_total)


def backward_factors(d_embed, embedding, inverse, pre_conv, pre_pool, w_conv, grad_scale):
    width = embedding.shape[1]
    radial = jnp.sum(d_embed * embedding, axis=1, keepdims=True)
    d_pre_conv = silu_slope(pre_conv) * inverse * (d_embed - embedding * radial) * grad_scale
    d_conv_b = d_pre_conv.astype(jnp.bfloat16)
    grad_conv_b = jnp.sum(d_pre_conv, axis=0)
    d_neighbour = lax.dot_general(
        d_conv_b, w_conv[width:], (((1,), (1,)), ((), ())), preferred_element_type=jnp.float32
    )
    d_pre_pool = silu_slope(pre_pool) * d_neighbour
    d_pool_b = d_pre_pool.astype(jnp.bfloat16)
    grad_pool_b = jnp.sum(d_pre_pool, axis=0)
    return (d_conv_b, d_pool_b, grad_pool_b, grad_conv_b)


def weight_grads(joined, pooled_b, d_conv_b, d_pool_b, stats):
    owners = lax.axis_size(OWNER)
    queries = joined.shape[0]
    conv_rows = joined.shape[1] // owners
    pool_rows = pooled_b.shape[1] // owners
    left = jnp.concatenate(
        [
            joined.reshape(queries, owners, conv_rows).transpose(1, 0, 2),
            pooled_b.reshape(queries, owners, pool_rows).transpose(1, 0, 2),
        ],
        axis=2,
    )
    left = lax.all_to_all(left, OWNER, split_axis=0, concat_axis=0, tiled=True)
    stats_hi = stats.astype(jnp.bfloat16)
    stats_lo = (stats - stats_hi.astype(jnp.float32)).astype(jnp.bfloat16)
    payload = jnp.concatenate([d_conv_b, d_pool_b], axis=1)
    payload = jnp.concatenate([payload, stats_hi, stats_lo], axis=0)
    gathered = lax.all_gather(payload, OWNER[2], axis=0)
    gathered = lax.all_gather(gathered, OWNER[1], axis=0)
    ring = ring_gather(gathered, OWNER[0], lax.axis_size(OWNER[0]))
    here = lax.axis_index(OWNER[0])
    left = jnp.roll(left.reshape((ring.shape[0], -1) + left.shape[1:]), -here, axis=0)
    left = left.reshape(owners * queries, conv_rows + pool_rows)
    right = ring[:, :, :, :queries].reshape(owners * queries, payload.shape[1])
    stat_rows = stats.shape[0]
    stat_parts = jnp.roll(ring[:, :, :, queries:], here, axis=0).astype(jnp.float32)
    stats_sum = jnp.sum(
        stat_parts[:, :, :, :stat_rows] + stat_parts[:, :, :, stat_rows:], axis=(0, 1, 2)
    )
    contract_rows = (((0,), (0,)), ((), ()))
    conv_width = d_conv_b.shape[1]
    conv_part = lax.dot_general(
        left[:, :conv_rows], right[:, :conv_width], contract_rows,
        preferred_element_type=jnp.float32,
    )
    pool_part = lax.dot_general(
        left[:, conv_rows:], right[:, conv_width:], contract_rows,
        preferred_element_type=jnp.float32,
    )
    return pool_part, conv_part, stats_sum


def ring_gather(block, axis, size):
    ahead, behind = [], []
    forward_part, backward_part = block, block
    for step in range(1, size // 2 + 1):
        forward_part = lax.ppermute(forward_part, axis, [(i, (i + 1) % size) for i in range(size)])
        behind.append(forward_part)
        if 2 * step < size:
            backward_part = lax.ppermute(backward_part, axis, [(i, (i - 1) % size) for i in range(size)])
            ahead.append(backward_part)
    return jnp.stack([block] + ahead + behind[::-1])


def pair_sum(values, groups):
    step = 1
    while step < groups:
        partner = lax.ppermute(values, "neg", [(i, i ^ step) for i in range(groups)])
        values = values + partner
        step *= 2
    return values


def bucket(page_list, owners, rows_per, capacity):
    count = page_list.shape[0]
    owner_of = page_list // rows_per
    local_row = page_list - owner_of * rows_per
    one_hot = (owner_of[:, None] == jnp.arange(owners, dtype=jnp.int32)[None, :]).astype(jnp.bfloat16)
    positions = jnp.arange(count, dtype=jnp.int32)
    earlier = (positions[:, None] > positions[None, :]).astype(jnp.bfloat16)
    before = jnp.dot(earlier, one_hot, preferred_element_type=jnp.float32)
    slot_of = jnp.sum(before * one_hot.astype(jnp.float32), axis=1).astype(jnp.int32)
    flat = owner_of * capacity + slot_of
    select = (flat[:, None] == jnp.arange(owners * capacity, dtype=jnp.int32)[None, :]).astype(jnp.bfloat16)
    parts = jnp.stack([local_row // 64, local_row % 64]).astype(jnp.bfloat16)
    placed = jnp.dot(parts, select, preferred_element_type=jnp.float32).astype(jnp.int32)
    requests = (placed[0] * 64 + placed[1]).reshape(owners, capacity)
    return (owner_of, slot_of, requests)


def local(nbr_ids, visit_counts, self_ids, pos_ids, neg_ids, table, w_pool, b_pool, w_conv, b_conv):
    owners = lax.axis_size(OWNER)
    groups = lax.axis_size("neg")
    rows_per = table.shape[0]
    width = table.shape[1]
    queries, fan_count = nbr_ids.shape
    neg_count = neg_ids.shape[1]
    counts_f = visit_counts.astype(jnp.float32)
    weights = counts_f / jnp.sum(counts_f, axis=1, keepdims=True)
    flat_ids = nbr_ids.reshape(-1)
    capacity = 2 * (flat_ids.shape[0] // owners) + 4
    page_cap = 2 * (queries * (neg_count + 2) // owners) + 4
    capacity = -(-capacity // 8) * 8
    page_cap = -(-page_cap // 8) * 8
    total_queries = queries * owners * groups
    grad_scale = 1.0 / neg_count
    loss_scale = 1.0 / (total_queries * neg_count)
    owner_of, slot_of, requests = bucket(flat_ids, owners, rows_per, capacity)
    page_list = jnp.concatenate([self_ids, pos_ids, neg_ids.reshape(-1)])
    page_owner, page_slot, page_requests = bucket(page_list, owners, rows_per, page_cap)
    slots = capacity + page_cap
    all_requests = jnp.concatenate([requests, page_requests], axis=1)
    served = lax.all_to_all(all_requests, OWNER, split_axis=0, concat_axis=0, tiled=True)
    nbr_rows = lax.all_to_all(
        table[served[:, :capacity].reshape(-1)].reshape(owners, capacity, width),
        OWNER, split_axis=0, concat_axis=0, tiled=True,
    ).reshape(owners * capacity, width)
    page_rows = lax.all_to_all(
        table[served[:, capacity:].reshape(-1)].reshape(owners, page_cap, width),
        OWNER, split_axis=0, concat_axis=0, tiled=True,
    ).reshape(owners * page_cap, width)
    nbr_flat = (owner_of * capacity + slot_of).reshape(queries, fan_count)
    nbr_slots = jnp.arange(owners * capacity, dtype=jnp.int32)
    pool_weights = jnp.sum(
        jnp.where(nbr_flat[:, :, None] == nbr_slots[None, None, :], weights[:, :, None], 0.0), axis=1
    )
    pooled = jnp.dot(
        pool_weights, nbr_rows.astype(jnp.float32), precision=lax.Precision.HIGHEST,
        preferred_element_type=jnp.float32,
    )
    page_flat = page_owner * page_cap + page_slot
    page_slots = jnp.arange(owners * page_cap, dtype=jnp.int32)
    self_flat = page_flat[:queries]
    pos_flat = page_flat[queries : 2 * queries]
    neg_flat = page_flat[2 * queries :].reshape(queries, neg_count)
    pick = (jnp.stack([self_flat, pos_flat])[:, :, None] == page_slots[None, None, :]).astype(jnp.bfloat16)
    picked = jnp.einsum("aqs,se->aqe", pick, page_rows, preferred_element_type=jnp.float32)
    self_rows = picked[0].astype(jnp.bfloat16)
    pos_rows = picked[1].astype(jnp.bfloat16)
    pooled_b, pre_pool, joined, pre_conv, inverse, embedding = forward(
        pooled, self_rows, w_pool, b_pool, w_conv, b_conv
    )
    embed_b = embedding.astype(jnp.bfloat16)
    slot_scores = lax.dot_general(
        embed_b, page_rows, (((1,), (1,)), ((), ())), preferred_element_type=jnp.float32
    )
    neg_match = neg_flat[:, :, None] == page_slots[None, None, :]
    neg_scores = jnp.sum(jnp.where(neg_match, slot_scores[:, None, :], 0.0), axis=2)
    pos_scores = jnp.einsum("qe,qe->q", embed_b, pos_rows, preferred_element_type=jnp.float32)
    loss_part, slope_b, slope_total = margin_terms(neg_scores, pos_scores, loss_scale)
    slope_slots = jnp.sum(
        jnp.where(
            neg_match,
            slope_b.astype(jnp.float32)[:, :, None],
            0.0,
        ),
        axis=1,
    ).astype(jnp.bfloat16)
    d_embed = jnp.dot(
        slope_slots, page_rows, preferred_element_type=jnp.float32
    ) - slope_total * pos_rows.astype(jnp.float32)
    d_conv_b, d_pool_b, pool_bgrad, conv_bgrad = backward_factors(
        d_embed, embedding, inverse, pre_conv, pre_pool, w_conv, grad_scale
    )
    loss_row = jnp.zeros((2 * width,), jnp.float32).at[0].set(loss_part)
    stats = jnp.stack([jnp.concatenate([conv_bgrad, pool_bgrad]), loss_row])
    pool_part, conv_part, stats_sum = weight_grads(joined, pooled_b, d_conv_b, d_pool_b, stats)
    pool_rows = pool_part.shape[0]
    conv_rows = conv_part.shape[0]
    summed = pair_sum(
        jnp.concatenate([pool_part, conv_part, stats_sum.reshape(-1, width)], axis=0), groups
    )
    grad_pool_w = summed[:pool_rows]
    grad_conv_w = summed[pool_rows : pool_rows + conv_rows]
    stats_all = summed[pool_rows + conv_rows :].reshape(stats_sum.shape)
    grad_conv_b = stats_all[0, :width]
    grad_pool_b = stats_all[0, width:]
    loss_sum = stats_all[1, 0]
    return (embedding, loss_sum, grad_pool_w, grad_pool_b, grad_conv_w, grad_conv_b)


def solution(mesh):
    owners, groups = mesh.devices.shape
    cores = 2
    rows_y = 4 if owners % (cores * 4) == 0 else 1
    fine = Mesh(
        mesh.devices.reshape(owners // (cores * rows_y), rows_y, cores, groups),
        OWNER + ("neg",),
    )
    spread = OWNER + ("neg",)
    return jax.shard_map(
        local,
        mesh=fine,
        in_specs=(
            P(spread, None),
            P(spread, None),
            P(spread),
            P(spread),
            P(spread, None),
            P(OWNER, None),
            P(),
            P(),
            P(),
            P(),
        ),
        out_specs=(P(spread, None), P(), P(OWNER, None), P(), P(OWNER, None), P()),
        check_vma=False,
    )
```

```python
import jax
import jax.numpy as jnp
from jax import lax
from jax.sharding import Mesh, PartitionSpec as P

margin_value = 0.5
OWNER = ("oz", "oy", "oc")


def silu_slope(values):
    sig = jax.nn.sigmoid(values)
    return sig * (1.0 + values * (1.0 - sig))


def forward(pooled, self_rows, w_pool, b_pool, w_conv, b_conv):
    pooled_b = pooled.astype(jnp.bfloat16)
    pre_pool = jnp.dot(pooled_b, w_pool, preferred_element_type=jnp.float32) + b_pool
    neighbour = jax.nn.silu(pre_pool).astype(jnp.bfloat16)
    joined = jnp.concatenate([self_rows, neighbour], axis=1)
    pre_conv = jnp.dot(joined, w_conv, preferred_element_type=jnp.float32) + b_conv
    hidden = jax.nn.silu(pre_conv)
    inverse = lax.rsqrt(jnp.sum(hidden * hidden, axis=1, keepdims=True) + 1e-05)
    embedding = hidden * inverse
    return (pooled_b, pre_pool, joined, pre_conv, inverse, embedding)


def margin_terms(neg_scores, pos_scores, loss_scale):
    margins = neg_scores - pos_scores[:, None] + margin_value
    loss_part = jnp.sum(jax.nn.softplus(margins)) * loss_scale
    slope_b = jax.nn.sigmoid(margins).astype(jnp.bfloat16)
    slope_total = jnp.sum(slope_b.astype(jnp.float32), axis=1, keepdims=True)
    return (loss_part, slope_b, slope_total)


def backward_factors(d_embed, embedding, inverse, pre_conv, pre_pool, w_conv, grad_scale):
    width = embedding.shape[1]
    radial = jnp.sum(d_embed * embedding, axis=1, keepdims=True)
    d_pre_conv = silu_slope(pre_conv) * inverse * (d_embed - embedding * radial) * grad_scale
    d_conv_b = d_pre_conv.astype(jnp.bfloat16)
    grad_conv_b = jnp.sum(d_pre_conv, axis=0)
    d_neighbour = lax.dot_general(
        d_conv_b, w_conv[width:], (((1,), (1,)), ((), ())), preferred_element_type=jnp.float32
    )
    d_pre_pool = silu_slope(pre_pool) * d_neighbour
    d_pool_b = d_pre_pool.astype(jnp.bfloat16)
    grad_pool_b = jnp.sum(d_pre_pool, axis=0)
    return (d_conv_b, d_pool_b, grad_pool_b, grad_conv_b)


def weight_grads(joined, pooled_b, d_conv_b, d_pool_b, stats):
    owners = lax.axis_size(OWNER)
    queries = joined.shape[0]
    conv_rows = joined.shape[1] // owners
    pool_rows = pooled_b.shape[1] // owners
    left = jnp.concatenate(
        [
            joined.reshape(queries, owners, conv_rows).transpose(1, 0, 2),
            pooled_b.reshape(queries, owners, pool_rows).transpose(1, 0, 2),
        ],
        axis=2,
    )
    loss_value = stats[1, 0]
    loss_hi = loss_value.astype(jnp.bfloat16)
    loss_lo = (loss_value - loss_hi.astype(jnp.float32)).astype(jnp.bfloat16)
    loss_chunk = jnp.zeros((owners, 1, left.shape[2]), jnp.bfloat16)
    loss_chunk = loss_chunk.at[:, 0, 0].set(loss_hi).at[:, 0, 1].set(loss_lo)
    left = jnp.concatenate([left, loss_chunk], axis=1)
    left = lax.all_to_all(left, OWNER, split_axis=0, concat_axis=0, tiled=True)
    loss_parts = left[:, queries, :2].astype(jnp.float32)
    loss_owner = jnp.sum(loss_parts[:, 0] + loss_parts[:, 1])
    left = left[:, :queries]
    bias_stats = stats[:1]
    stats_hi = bias_stats.astype(jnp.bfloat16)
    stats_lo = (bias_stats - stats_hi.astype(jnp.float32)).astype(jnp.bfloat16)
    payload = jnp.concatenate([d_conv_b, d_pool_b], axis=1)
    payload = jnp.concatenate([payload, stats_hi, stats_lo], axis=0)
    gathered = lax.all_gather(payload, OWNER[2], axis=0)
    gathered = lax.all_gather(gathered, OWNER[1], axis=0)
    ring = ring_gather(gathered, OWNER[0], lax.axis_size(OWNER[0]))
    here = lax.axis_index(OWNER[0])
    left = jnp.roll(left.reshape((ring.shape[0], -1) + left.shape[1:]), -here, axis=0)
    left = left.reshape(owners * queries, conv_rows + pool_rows)
    right = ring[:, :, :, :queries].reshape(owners * queries, payload.shape[1])
    stat_rows = bias_stats.shape[0]
    stat_parts = jnp.roll(ring[:, :, :, queries:], here, axis=0).astype(jnp.float32)
    stats_sum = jnp.sum(
        stat_parts[:, :, :, :stat_rows] + stat_parts[:, :, :, stat_rows:], axis=(0, 1, 2)
    )
    loss_line = jnp.zeros((1, stats.shape[1]), jnp.float32).at[0, 0].set(loss_owner)
    stats_sum = jnp.concatenate([stats_sum, loss_line], axis=0)
    contract_rows = (((0,), (0,)), ((), ()))
    conv_width = d_conv_b.shape[1]
    conv_part = lax.dot_general(
        left[:, :conv_rows], right[:, :conv_width], contract_rows,
        preferred_element_type=jnp.float32,
    )
    pool_part = lax.dot_general(
        left[:, conv_rows:], right[:, conv_width:], contract_rows,
        preferred_element_type=jnp.float32,
    )
    return pool_part, conv_part, stats_sum


def ring_gather(block, axis, size):
    ahead, behind = [], []
    forward_part, backward_part = block, block
    for step in range(1, size // 2 + 1):
        forward_part = lax.ppermute(forward_part, axis, [(i, (i + 1) % size) for i in range(size)])
        behind.append(forward_part)
        if 2 * step < size:
            backward_part = lax.ppermute(backward_part, axis, [(i, (i - 1) % size) for i in range(size)])
            ahead.append(backward_part)
    return jnp.stack([block] + ahead + behind[::-1])


def pair_sum(values, groups):
    step = 1
    while step < groups:
        partner = lax.ppermute(values, "neg", [(i, i ^ step) for i in range(groups)])
        values = values + partner
        step *= 2
    return values


def bucket(page_list, owners, rows_per, capacity):
    count = page_list.shape[0]
    owner_of = page_list // rows_per
    local_row = page_list - owner_of * rows_per
    one_hot = (owner_of[:, None] == jnp.arange(owners, dtype=jnp.int32)[None, :]).astype(jnp.bfloat16)
    positions = jnp.arange(count, dtype=jnp.int32)
    earlier = (positions[:, None] > positions[None, :]).astype(jnp.bfloat16)
    before = jnp.dot(earlier, one_hot, preferred_element_type=jnp.float32)
    slot_of = jnp.sum(before * one_hot.astype(jnp.float32), axis=1).astype(jnp.int32)
    flat = owner_of * capacity + slot_of
    select = (flat[:, None] == jnp.arange(owners * capacity, dtype=jnp.int32)[None, :]).astype(jnp.bfloat16)
    parts = jnp.stack([local_row // 64, local_row % 64]).astype(jnp.bfloat16)
    placed = jnp.dot(parts, select, preferred_element_type=jnp.float32).astype(jnp.int32)
    requests = (placed[0] * 64 + placed[1]).reshape(owners, capacity)
    return (owner_of, slot_of, requests)


def local(nbr_ids, visit_counts, self_ids, pos_ids, neg_ids, table, w_pool, b_pool, w_conv, b_conv):
    owners = lax.axis_size(OWNER)
    groups = lax.axis_size("neg")
    rows_per = table.shape[0]
    width = table.shape[1]
    queries, fan_count = nbr_ids.shape
    neg_count = neg_ids.shape[1]
    counts_f = visit_counts.astype(jnp.float32)
    weights = counts_f / jnp.sum(counts_f, axis=1, keepdims=True)
    flat_ids = nbr_ids.reshape(-1)
    capacity = 2 * (flat_ids.shape[0] // owners) + 4
    page_cap = 2 * (queries * (neg_count + 2) // owners) + 4
    capacity = -(-capacity // 8) * 8
    page_cap = -(-page_cap // 8) * 8
    total_queries = queries * owners * groups
    grad_scale = 1.0 / neg_count
    loss_scale = 1.0 / (total_queries * neg_count)
    owner_of, slot_of, requests = bucket(flat_ids, owners, rows_per, capacity)
    page_list = jnp.concatenate([self_ids, pos_ids, neg_ids.reshape(-1)])
    page_owner, page_slot, page_requests = bucket(page_list, owners, rows_per, page_cap)
    slots = capacity + page_cap
    all_requests = jnp.concatenate([requests, page_requests], axis=1)
    served = lax.all_to_all(all_requests, OWNER, split_axis=0, concat_axis=0, tiled=True)
    nbr_rows = lax.all_to_all(
        table[served[:, :capacity].reshape(-1)].reshape(owners, capacity, width),
        OWNER, split_axis=0, concat_axis=0, tiled=True,
    ).reshape(owners * capacity, width)
    page_rows = lax.all_to_all(
        table[served[:, capacity:].reshape(-1)].reshape(owners, page_cap, width),
        OWNER, split_axis=0, concat_axis=0, tiled=True,
    ).reshape(owners * page_cap, width)
    nbr_flat = (owner_of * capacity + slot_of).reshape(queries, fan_count)
    nbr_slots = jnp.arange(owners * capacity, dtype=jnp.int32)
    pool_weights = jnp.sum(
        jnp.where(nbr_flat[:, :, None] == nbr_slots[None, None, :], weights[:, :, None], 0.0), axis=1
    )
    pooled = jnp.dot(
        pool_weights, nbr_rows.astype(jnp.float32), precision=lax.Precision.HIGHEST,
        preferred_element_type=jnp.float32,
    )
    page_flat = page_owner * page_cap + page_slot
    page_slots = jnp.arange(owners * page_cap, dtype=jnp.int32)
    self_flat = page_flat[:queries]
    pos_flat = page_flat[queries : 2 * queries]
    neg_flat = page_flat[2 * queries :].reshape(queries, neg_count)
    pick = (jnp.stack([self_flat, pos_flat])[:, :, None] == page_slots[None, None, :]).astype(jnp.bfloat16)
    picked = jnp.einsum("aqs,se->aqe", pick, page_rows, preferred_element_type=jnp.float32)
    self_rows = picked[0].astype(jnp.bfloat16)
    pos_rows = picked[1].astype(jnp.bfloat16)
    pooled_b, pre_pool, joined, pre_conv, inverse, embedding = forward(
        pooled, self_rows, w_pool, b_pool, w_conv, b_conv
    )
    embed_b = embedding.astype(jnp.bfloat16)
    slot_scores = lax.dot_general(
        embed_b, page_rows, (((1,), (1,)), ((), ())), preferred_element_type=jnp.float32
    )
    neg_match = neg_flat[:, :, None] == page_slots[None, None, :]
    neg_scores = jnp.sum(jnp.where(neg_match, slot_scores[:, None, :], 0.0), axis=2)
    pos_scores = jnp.einsum("qe,qe->q", embed_b, pos_rows, preferred_element_type=jnp.float32)
    loss_part, slope_b, slope_total = margin_terms(neg_scores, pos_scores, loss_scale)
    slope_slots = jnp.sum(
        jnp.where(
            neg_match,
            slope_b.astype(jnp.float32)[:, :, None],
            0.0,
        ),
        axis=1,
    ).astype(jnp.bfloat16)
    d_embed = jnp.dot(
        slope_slots, page_rows, preferred_element_type=jnp.float32
    ) - slope_total * pos_rows.astype(jnp.float32)
    d_conv_b, d_pool_b, pool_bgrad, conv_bgrad = backward_factors(
        d_embed, embedding, inverse, pre_conv, pre_pool, w_conv, grad_scale
    )
    loss_row = jnp.zeros((2 * width,), jnp.float32).at[0].set(loss_part)
    stats = jnp.stack([jnp.concatenate([conv_bgrad, pool_bgrad]), loss_row])
    pool_part, conv_part, stats_sum = weight_grads(joined, pooled_b, d_conv_b, d_pool_b, stats)
    pool_rows = pool_part.shape[0]
    conv_rows = conv_part.shape[0]
    summed = pair_sum(
        jnp.concatenate([pool_part, conv_part, stats_sum.reshape(-1, width)], axis=0), groups
    )
    grad_pool_w = summed[:pool_rows]
    grad_conv_w = summed[pool_rows : pool_rows + conv_rows]
    stats_all = summed[pool_rows + conv_rows :].reshape(stats_sum.shape)
    grad_conv_b = stats_all[0, :width]
    grad_pool_b = stats_all[0, width:]
    loss_sum = stats_all[1, 0]
    return (embedding, loss_sum, grad_pool_w, grad_pool_b, grad_conv_w, grad_conv_b)


def solution(mesh):
    owners, groups = mesh.devices.shape
    cores = 2
    rows_y = 4 if owners % (cores * 4) == 0 else 1
    fine = Mesh(
        mesh.devices.reshape(owners // (cores * rows_y), rows_y, cores, groups),
        OWNER + ("neg",),
    )
    spread = OWNER + ("neg",)
    return jax.shard_map(
        local,
        mesh=fine,
        in_specs=(
            P(spread, None),
            P(spread, None),
            P(spread),
            P(spread),
            P(spread, None),
            P(OWNER, None),
            P(),
            P(),
            P(),
            P(),
        ),
        out_specs=(P(spread, None), P(), P(OWNER, None), P(), P(OWNER, None), P()),
        check_vma=False,
    )
```

```python
import jax
import jax.numpy as jnp
from jax import lax
from jax.sharding import Mesh, PartitionSpec as P

margin_value = 0.5
OWNER = ("oz", "oy", "oc")


def silu_slope(values):
    sig = jax.nn.sigmoid(values)
    return sig * (1.0 + values * (1.0 - sig))


def forward(pooled, self_rows, w_pool, b_pool, w_conv, b_conv):
    pooled_b = pooled.astype(jnp.bfloat16)
    pre_pool = jnp.dot(pooled_b, w_pool, preferred_element_type=jnp.float32) + b_pool
    neighbour = jax.nn.silu(pre_pool).astype(jnp.bfloat16)
    joined = jnp.concatenate([self_rows, neighbour], axis=1)
    pre_conv = jnp.dot(joined, w_conv, preferred_element_type=jnp.float32) + b_conv
    hidden = jax.nn.silu(pre_conv)
    inverse = lax.rsqrt(jnp.sum(hidden * hidden, axis=1, keepdims=True) + 1e-05)
    embedding = hidden * inverse
    return (pooled_b, pre_pool, joined, pre_conv, inverse, embedding)


def margin_terms(neg_scores, pos_scores, loss_scale):
    margins = neg_scores - pos_scores[:, None] + margin_value
    loss_part = jnp.sum(jax.nn.softplus(margins)) * loss_scale
    slope_b = jax.nn.sigmoid(margins).astype(jnp.bfloat16)
    slope_total = jnp.sum(slope_b.astype(jnp.float32), axis=1, keepdims=True)
    return (loss_part, slope_b, slope_total)


def backward_factors(d_embed, embedding, inverse, pre_conv, pre_pool, w_conv, grad_scale):
    width = embedding.shape[1]
    radial = jnp.sum(d_embed * embedding, axis=1, keepdims=True)
    d_pre_conv = silu_slope(pre_conv) * inverse * (d_embed - embedding * radial) * grad_scale
    d_conv_b = d_pre_conv.astype(jnp.bfloat16)
    grad_conv_b = jnp.sum(d_pre_conv, axis=0)
    d_neighbour = lax.dot_general(
        d_conv_b, w_conv[width:], (((1,), (1,)), ((), ())), preferred_element_type=jnp.float32
    )
    d_pre_pool = silu_slope(pre_pool) * d_neighbour
    d_pool_b = d_pre_pool.astype(jnp.bfloat16)
    grad_pool_b = jnp.sum(d_pre_pool, axis=0)
    return (d_conv_b, d_pool_b, grad_pool_b, grad_conv_b)


def weight_grads(joined, pooled_b, d_conv_b, d_pool_b, stats):
    owners = lax.axis_size(OWNER)
    queries = joined.shape[0]
    conv_rows = joined.shape[1] // owners
    pool_rows = pooled_b.shape[1] // owners
    left = jnp.concatenate(
        [
            joined.reshape(queries, owners, conv_rows).transpose(1, 0, 2),
            pooled_b.reshape(queries, owners, pool_rows).transpose(1, 0, 2),
        ],
        axis=2,
    )
    left = lax.all_to_all(left, OWNER, split_axis=0, concat_axis=0, tiled=True)
    stats_hi = stats.astype(jnp.bfloat16)
    stats_lo = (stats - stats_hi.astype(jnp.float32)).astype(jnp.bfloat16)
    payload = jnp.concatenate([d_conv_b, d_pool_b], axis=1)
    payload = jnp.concatenate([payload, stats_hi, stats_lo], axis=0)
    gathered = lax.all_gather(payload, OWNER[2], axis=0)
    gathered = lax.all_gather(gathered, OWNER[1], axis=0)
    ring = ring_gather(gathered, OWNER[0], lax.axis_size(OWNER[0]))
    here = lax.axis_index(OWNER[0])
    ring_size = len(ring)
    left = left.reshape((ring_size, -1) + left.shape[1:])
    stat_rows = stats.shape[0]
    stat_parts = jnp.roll(
        jnp.stack([part[:, :, queries:] for part in ring]), here, axis=0
    ).astype(jnp.float32)
    stats_sum = jnp.sum(
        stat_parts[:, :, :, :stat_rows] + stat_parts[:, :, :, stat_rows:], axis=(0, 1, 2)
    )
    contract_rows = (((0,), (0,)), ((), ()))
    conv_width = d_conv_b.shape[1]
    conv_part = 0.0
    pool_part = 0.0
    for step, part in enumerate(ring):
        block_left = lax.dynamic_index_in_dim(left, (here + step) % ring_size, 0, keepdims=False)
        block_left = block_left.reshape(-1, conv_rows + pool_rows)
        block_right = part[:, :, :queries].reshape(-1, payload.shape[1])
        conv_part = conv_part + lax.dot_general(
            block_left[:, :conv_rows], block_right[:, :conv_width], contract_rows,
            preferred_element_type=jnp.float32,
        )
        pool_part = pool_part + lax.dot_general(
            block_left[:, conv_rows:], block_right[:, conv_width:], contract_rows,
            preferred_element_type=jnp.float32,
        )
    return pool_part, conv_part, stats_sum


def ring_gather(block, axis, size):
    ahead, behind = [], []
    forward_part, backward_part = block, block
    for step in range(1, size // 2 + 1):
        forward_part = lax.ppermute(forward_part, axis, [(i, (i + 1) % size) for i in range(size)])
        behind.append(forward_part)
        if 2 * step < size:
            backward_part = lax.ppermute(backward_part, axis, [(i, (i - 1) % size) for i in range(size)])
            ahead.append(backward_part)
    return [block] + ahead + behind[::-1]


def pair_sum(values, groups):
    step = 1
    while step < groups:
        partner = lax.ppermute(values, "neg", [(i, i ^ step) for i in range(groups)])
        values = values + partner
        step *= 2
    return values


def bucket(page_list, owners, rows_per, capacity):
    count = page_list.shape[0]
    owner_of = page_list // rows_per
    local_row = page_list - owner_of * rows_per
    one_hot = (owner_of[:, None] == jnp.arange(owners, dtype=jnp.int32)[None, :]).astype(jnp.bfloat16)
    positions = jnp.arange(count, dtype=jnp.int32)
    earlier = (positions[:, None] > positions[None, :]).astype(jnp.bfloat16)
    before = jnp.dot(earlier, one_hot, preferred_element_type=jnp.float32)
    slot_of = jnp.sum(before * one_hot.astype(jnp.float32), axis=1).astype(jnp.int32)
    flat = owner_of * capacity + slot_of
    select = (flat[:, None] == jnp.arange(owners * capacity, dtype=jnp.int32)[None, :]).astype(jnp.bfloat16)
    parts = jnp.stack([local_row // 64, local_row % 64]).astype(jnp.bfloat16)
    placed = jnp.dot(parts, select, preferred_element_type=jnp.float32).astype(jnp.int32)
    requests = (placed[0] * 64 + placed[1]).reshape(owners, capacity)
    return (owner_of, slot_of, requests)


def local(nbr_ids, visit_counts, self_ids, pos_ids, neg_ids, table, w_pool, b_pool, w_conv, b_conv):
    owners = lax.axis_size(OWNER)
    groups = lax.axis_size("neg")
    rows_per = table.shape[0]
    width = table.shape[1]
    queries, fan_count = nbr_ids.shape
    neg_count = neg_ids.shape[1]
    counts_f = visit_counts.astype(jnp.float32)
    weights = counts_f / jnp.sum(counts_f, axis=1, keepdims=True)
    flat_ids = nbr_ids.reshape(-1)
    capacity = 2 * (flat_ids.shape[0] // owners) + 4
    page_cap = 2 * (queries * (neg_count + 2) // owners) + 4
    capacity = -(-capacity // 8) * 8
    page_cap = -(-page_cap // 8) * 8
    total_queries = queries * owners * groups
    grad_scale = 1.0 / neg_count
    loss_scale = 1.0 / (total_queries * neg_count)
    owner_of, slot_of, requests = bucket(flat_ids, owners, rows_per, capacity)
    page_list = jnp.concatenate([self_ids, pos_ids, neg_ids.reshape(-1)])
    page_owner, page_slot, page_requests = bucket(page_list, owners, rows_per, page_cap)
    slots = capacity + page_cap
    all_requests = jnp.concatenate([requests, page_requests], axis=1)
    served = lax.all_to_all(all_requests, OWNER, split_axis=0, concat_axis=0, tiled=True)
    nbr_rows = lax.all_to_all(
        table[served[:, :capacity].reshape(-1)].reshape(owners, capacity, width),
        OWNER, split_axis=0, concat_axis=0, tiled=True,
    ).reshape(owners * capacity, width)
    page_rows = lax.all_to_all(
        table[served[:, capacity:].reshape(-1)].reshape(owners, page_cap, width),
        OWNER, split_axis=0, concat_axis=0, tiled=True,
    ).reshape(owners * page_cap, width)
    nbr_flat = (owner_of * capacity + slot_of).reshape(queries, fan_count)
    nbr_slots = jnp.arange(owners * capacity, dtype=jnp.int32)
    pool_weights = jnp.sum(
        jnp.where(nbr_flat[:, :, None] == nbr_slots[None, None, :], weights[:, :, None], 0.0), axis=1
    )
    pooled = jnp.dot(
        pool_weights, nbr_rows.astype(jnp.float32), precision=lax.Precision.HIGHEST,
        preferred_element_type=jnp.float32,
    )
    page_flat = page_owner * page_cap + page_slot
    page_slots = jnp.arange(owners * page_cap, dtype=jnp.int32)
    self_flat = page_flat[:queries]
    pos_flat = page_flat[queries : 2 * queries]
    neg_flat = page_flat[2 * queries :].reshape(queries, neg_count)
    pick = (jnp.stack([self_flat, pos_flat])[:, :, None] == page_slots[None, None, :]).astype(jnp.bfloat16)
    picked = jnp.einsum("aqs,se->aqe", pick, page_rows, preferred_element_type=jnp.float32)
    self_rows = picked[0].astype(jnp.bfloat16)
    pos_rows = picked[1].astype(jnp.bfloat16)
    pooled_b, pre_pool, joined, pre_conv, inverse, embedding = forward(
        pooled, self_rows, w_pool, b_pool, w_conv, b_conv
    )
    embed_b = embedding.astype(jnp.bfloat16)
    slot_scores = lax.dot_general(
        embed_b, page_rows, (((1,), (1,)), ((), ())), preferred_element_type=jnp.float32
    )
    neg_match = neg_flat[:, :, None] == page_slots[None, None, :]
    neg_scores = jnp.sum(jnp.where(neg_match, slot_scores[:, None, :], 0.0), axis=2)
    pos_scores = jnp.einsum("qe,qe->q", embed_b, pos_rows, preferred_element_type=jnp.float32)
    loss_part, slope_b, slope_total = margin_terms(neg_scores, pos_scores, loss_scale)
    slope_slots = jnp.sum(
        jnp.where(
            neg_match,
            slope_b.astype(jnp.float32)[:, :, None],
            0.0,
        ),
        axis=1,
    ).astype(jnp.bfloat16)
    d_embed = jnp.dot(
        slope_slots, page_rows, preferred_element_type=jnp.float32
    ) - slope_total * pos_rows.astype(jnp.float32)
    d_conv_b, d_pool_b, pool_bgrad, conv_bgrad = backward_factors(
        d_embed, embedding, inverse, pre_conv, pre_pool, w_conv, grad_scale
    )
    loss_row = jnp.zeros((2 * width,), jnp.float32).at[0].set(loss_part)
    stats = jnp.stack([jnp.concatenate([conv_bgrad, pool_bgrad]), loss_row])
    pool_part, conv_part, stats_sum = weight_grads(joined, pooled_b, d_conv_b, d_pool_b, stats)
    pool_rows = pool_part.shape[0]
    conv_rows = conv_part.shape[0]
    summed = pair_sum(
        jnp.concatenate([pool_part, conv_part, stats_sum.reshape(-1, width)], axis=0), groups
    )
    grad_pool_w = summed[:pool_rows]
    grad_conv_w = summed[pool_rows : pool_rows + conv_rows]
    stats_all = summed[pool_rows + conv_rows :].reshape(stats_sum.shape)
    grad_conv_b = stats_all[0, :width]
    grad_pool_b = stats_all[0, width:]
    loss_sum = stats_all[1, 0]
    return (embedding, loss_sum, grad_pool_w, grad_pool_b, grad_conv_w, grad_conv_b)


def solution(mesh):
    owners, groups = mesh.devices.shape
    cores = 2
    rows_y = 4 if owners % (cores * 4) == 0 else 1
    fine = Mesh(
        mesh.devices.reshape(owners // (cores * rows_y), rows_y, cores, groups),
        OWNER + ("neg",),
    )
    spread = OWNER + ("neg",)
    return jax.shard_map(
        local,
        mesh=fine,
        in_specs=(
            P(spread, None),
            P(spread, None),
            P(spread),
            P(spread),
            P(spread, None),
            P(OWNER, None),
            P(),
            P(),
            P(),
            P(),
        ),
        out_specs=(P(spread, None), P(), P(OWNER, None), P(), P(OWNER, None), P()),
        check_vma=False,
    )
```
